256 devices in a mesh: ctx: 32 (over x, z_lo, core), tp: 8 (over z_hi, y).
Axes of the slice: x: 4, y: 4, z: 8 (z_hi: 2, z_lo: 4; z = z_hi * 4 + z_lo), core: 2. Of those that a mesh axis runs over, the one named last changes fastest.
Arguments:
- queries: bfloat16 [8192, 8192], P('ctx', 'tp'), may hold values from -8 to 8
- key_rows: bfloat16 [8192, 1024], P('ctx', 'tp'), may hold values from -8 to 8
- value_head_rows: bfloat16 [8192, 1024], P('ctx', 'tp'), may hold values from -6 to 6
- ssm_input: bfloat16 [8192, 8192], P('ctx', 'tp'), may hold values from -6 to 6
- gate_input: bfloat16 [8192, 8192], P('ctx', 'tp'), may hold values from -6 to 6
- b_matrix: bfloat16 [8192, 1024], P('ctx', 'tp'), may hold values from -6 to 6
- c_matrix: bfloat16 [8192, 1024], P('ctx', 'tp'), may hold values from -0.5 to 0.5
- step_size: float32 [128, 8192], P('tp', 'ctx'), may hold values from 0.02 to 0.2
- log_decay: float32 [128, 8192], P('tp', 'ctx'), may hold values from -1.5 to 0
- skip_gain: float32 [128], P('tp'), may hold values from 0.5 to 1.5
- norm_gain: bfloat16 [8192], P('tp'), may hold values from 0.099609375 to 1.8984375
Outputs:
- attention_out: bfloat16 [8192, 8192], P('ctx', 'tp')
- mixer_out: bfloat16 [8192, 8192], P('ctx', 'tp')
The draws below stay inside these ranges and needn't reach their ends.
All inputs are finite; a program needn't handle non-finite values.
Results may differ from the reference program's by a relative error of at most 0.022.
Values may be sent and summed in bfloat16 or wider, within the bound.
No kernel may reach another device: no remote copies, remote signals or barrier semaphores. Data moves between devices by JAX's collectives and lax.ppermute only.
A program may use at most 128 MiB of HBM per device.

```python
import math
import jax
import jax.numpy as jnp
from jax import lax

QUERY_HEADS = 64
KEY_VALUE_HEADS = 8
HEAD_WIDTH = 128
STATE_HEADS = 128
P_SIZE = 64
N = 128
GROUPS = 8
TOK_DEV = 256
SEQUENCE_TOKENS = 8192
INNER = 8192
N_CTX = 32


def draw_queries(key, part):
    sender_index = jax.random.fold_in(key, 11)
    sampled_values = 2.0 * jax.random.truncated_normal(sender_index, -4.0, 4.0, (SEQUENCE_TOKENS, QUERY_HEADS * HEAD_WIDTH), jnp.float32)
    return sampled_values.astype(jnp.bfloat16)


def draw_key_rows(key, part):
    sender_index = jax.random.fold_in(key, 13)
    sampled_values = jax.random.truncated_normal(sender_index, -6.0, 6.0, (SEQUENCE_TOKENS, KEY_VALUE_HEADS * HEAD_WIDTH), jnp.float32)
    return sampled_values.astype(jnp.bfloat16)


def draw_log_decay(key, part):
    random_subkeys = [jax.random.fold_in(key, 31 + offset) for offset in range(7)]
    slow_share = 0.5
    is_slow = jax.random.bernoulli(random_subkeys[0], slow_share, (STATE_HEADS, 1))
    slow_rate = jnp.exp(jax.random.uniform(random_subkeys[1], (STATE_HEADS, 1), jnp.float32, math.log(0.1), math.log(0.35))) / SEQUENCE_TOKENS
    fast_rate = jnp.exp(jax.random.uniform(random_subkeys[2], (STATE_HEADS, 1), jnp.float32, math.log(0.004), math.log(0.033)))
    per_block = jnp.exp(jax.random.uniform(random_subkeys[3], (STATE_HEADS, SEQUENCE_TOKENS // TOK_DEV), jnp.float32, math.log(0.5), math.log(2.0)))
    per_block = jnp.repeat(per_block, TOK_DEV, axis=1)
    roughness = jnp.exp(jax.random.uniform(random_subkeys[4], (STATE_HEADS, SEQUENCE_TOKENS), jnp.float32, math.log(0.6), math.log(1.6)))
    spike_start = jax.random.randint(random_subkeys[5], (STATE_HEADS, 2, 1), 0, SEQUENCE_TOKENS)
    spike_length = jax.random.uniform(random_subkeys[6], (STATE_HEADS, 2, 1), jnp.float32, 0.22, 0.69)
    token_index = jnp.arange(SEQUENCE_TOKENS)[None, None, :]
    spike_list = jnp.sum(jnp.where(token_index == spike_start, spike_length, 0.0), axis=1)
    decay_speed = jnp.where(is_slow, slow_rate, fast_rate) * per_block * roughness
    return -(decay_speed + spike_list)


def level_of(rng, dims, split, smallest, largest):
    gain, own = 1.0, jax.random.fold_in(rng, 6)
    for dim, shards_of in split:
        heights = jnp.exp(jax.random.uniform(jax.random.fold_in(own, dim), (shards_of,), jnp.float32, smallest / len(split), largest / len(split)))
        gain = gain * jnp.repeat(heights, dims[dim] // shards_of).reshape([-1 if axis == dim else 1 for axis in range(len(dims))])
    return gain


def noise(own_key, dims, scale, bound, shards=(), kind=jnp.bfloat16):
    array = jax.random.normal(own_key, dims, jnp.float32) * scale
    if len(shards) > 0:
        array = level_of(own_key, dims, shards, -0.22, 0.18) * array
    return jnp.clip(array, min=-bound, max=bound).astype(kind)


def setup_inputs(seed: int = 0) -> dict:
    seeds = jax.random.split(jax.random.key(seed), 12)
    queries = draw_queries(jax.random.fold_in(seeds[11], 71), 0)
    key_rows = draw_key_rows(jax.random.fold_in(seeds[11], 71), 0)
    value_head_rows = noise(seeds[2], (SEQUENCE_TOKENS, KEY_VALUE_HEADS * HEAD_WIDTH), 1.0, 6.0, ((0, 32), (1, 8)))
    ssm_input = noise(seeds[3], (SEQUENCE_TOKENS, INNER), 1.0, 6.0, ((0, 32), (1, 8)))
    gate_input = noise(seeds[4], (SEQUENCE_TOKENS, INNER), 1.0, 6.0, ((0, 32), (1, 8)))
    b_matrix = noise(seeds[5], (SEQUENCE_TOKENS, GROUPS * N), 1.0, 6.0, ((0, 32), (1, 8)))
    c_matrix = noise(seeds[6], (SEQUENCE_TOKENS, GROUPS * N), N ** -0.5, 0.5, ((0, 32), (1, 8)))
    step_size = jnp.clip(jnp.exp(math.log(0.2) - 2.3025851 * jax.random.uniform(seeds[7], (STATE_HEADS, SEQUENCE_TOKENS), jnp.float32) ** level_of(seeds[7], (STATE_HEADS, SEQUENCE_TOKENS), ((0, 8), (1, 32)), -0.2, 0.2)), 0.02, 0.2)
    log_decay = draw_log_decay(jax.random.fold_in(seeds[11], 71), 0)
    skip_gain = jnp.clip(0.5 + 1.0 * jax.random.uniform(seeds[9], (STATE_HEADS,), jnp.float32) ** level_of(seeds[9], (STATE_HEADS,), ((0, 8),), -0.2, 0.2), 0.5, 1.5)
    norm_gain = jnp.clip(1.0 + 0.18 * jax.random.normal(seeds[10], (INNER,), jnp.float32), 0.099609375, 1.8984375).astype(jnp.bfloat16)
    return {"queries": queries, "key_rows": key_rows, "value_head_rows": value_head_rows, "ssm_input": ssm_input, "gate_input": gate_input, "b_matrix": b_matrix, "c_matrix": c_matrix, "step_size": step_size, "log_decay": log_decay, "skip_gain": skip_gain, "norm_gain": norm_gain}


causal_score = -1e+30

def attention_part(queries, key_rows, value_head_rows):
    block_length = min(512, SEQUENCE_TOKENS)
    block_total = SEQUENCE_TOKENS // block_length
    query_per_key_heads = QUERY_HEADS // KEY_VALUE_HEADS
    score_factor = HEAD_WIDTH ** (-0.5)

    def query_block(block_id):
        q_start = block_id * block_length
        query_head_rows = lax.dynamic_slice_in_dim(queries, q_start, block_length, 0).astype(jnp.float32)
        query_head_rows = query_head_rows.reshape(block_length, KEY_VALUE_HEADS, query_per_key_heads, HEAD_WIDTH)
        query_pos = q_start + jnp.arange(block_length, dtype=jnp.int32)

        def key_step(key_block_id, running):
            run_max, run_sum, summed_so_far = running
            k_start = key_block_id * block_length
            key_portion = lax.dynamic_slice_in_dim(key_rows, k_start, block_length, 0).astype(jnp.float32)
            key_portion = key_portion.reshape(block_length, KEY_VALUE_HEADS, HEAD_WIDTH)
            value_portion = lax.dynamic_slice_in_dim(value_head_rows, k_start, block_length, 0).astype(jnp.float32)
            value_portion = value_portion.reshape(block_length, KEY_VALUE_HEADS, HEAD_WIDTH)
            key_pos = k_start + jnp.arange(block_length, dtype=jnp.int32)
            is_valid = key_pos[None, :] <= query_pos[:, None]
            score_matrix = jnp.einsum('faqo,bao->aqfb', query_head_rows, key_portion) * score_factor
            score_matrix = jnp.where(is_valid, score_matrix, causal_score)
            new_max = jnp.maximum(run_max, lax.optimization_barrier(jnp.max(score_matrix, axis=-1)))
            weights = jnp.where(is_valid, jnp.exp(score_matrix - new_max[..., None]), 0.0)
            correction_factor = jnp.exp(run_max - new_max)
            run_sum = run_sum * correction_factor + lax.optimization_barrier(jnp.sum(weights, axis=-1))
            quantized_values = lax.optimization_barrier(weights.astype(jnp.bfloat16)).astype(jnp.float32)
            summed_so_far = summed_so_far * correction_factor[..., None] + jnp.einsum('wlhc,cwm->wlhm', quantized_values, value_portion)
            return (new_max, run_sum, summed_so_far)
        starting_state = (jnp.full((KEY_VALUE_HEADS, query_per_key_heads, block_length), causal_score, jnp.float32), jnp.zeros((KEY_VALUE_HEADS, query_per_key_heads, block_length), jnp.float32), jnp.zeros((KEY_VALUE_HEADS, query_per_key_heads, block_length, HEAD_WIDTH), jnp.float32))
        run_max, run_sum, summed_so_far = lax.fori_loop(0, block_id + 1, key_step, starting_state)
        result = summed_so_far / run_sum[..., None]
        return result.transpose(2, 0, 1, 3).reshape(block_length, QUERY_HEADS * HEAD_WIDTH).astype(jnp.bfloat16)
    blocks_out = lax.map(query_block, jnp.arange(block_total, dtype=jnp.int32))
    return blocks_out.reshape(SEQUENCE_TOKENS, QUERY_HEADS * HEAD_WIDTH)

def mixer_part(ssm_input, gate_input, b_matrix, c_matrix, step_size, log_decay, skip_gain, norm_gain):
    heads_group = STATE_HEADS // GROUPS
    causal = jnp.tril(jnp.ones((TOK_DEV, TOK_DEV), dtype=bool))

    def ssm_block(carried, block_id):
        b_start = block_id * TOK_DEV
        mixer_in = lax.dynamic_slice_in_dim(ssm_input, b_start, TOK_DEV, 0).reshape(TOK_DEV, GROUPS, heads_group, P_SIZE)
        in_maps = lax.dynamic_slice_in_dim(b_matrix, b_start, TOK_DEV, 0).reshape(TOK_DEV, GROUPS, N)
        out_maps = lax.dynamic_slice_in_dim(c_matrix, b_start, TOK_DEV, 0).reshape(TOK_DEV, GROUPS, N)
        steps_here = lax.dynamic_slice_in_dim(step_size, b_start, TOK_DEV, 1).reshape(GROUPS, heads_group, TOK_DEV)
        decay_here = lax.dynamic_slice_in_dim(log_decay, b_start, TOK_DEV, 1).reshape(GROUPS, heads_group, TOK_DEV)
        cumul = jnp.cumsum(decay_here, axis=-1)
        mixer_f = mixer_in.astype(jnp.float32)
        out_f = out_maps.astype(jnp.float32)
        gram = jnp.einsum('tgn,sgn->gts', out_f, in_maps.astype(jnp.float32))
        spread = jnp.where(causal, cumul[..., :, None] - cumul[..., None, :], 0.0)
        mixing = jnp.where(causal, gram[:, None] * jnp.exp(spread) * steps_here[..., None, :], 0.0)
        mixing = lax.optimization_barrier(mixing.astype(jnp.bfloat16)).astype(jnp.float32)
        inner = jnp.einsum('ghts,sghp->tghp', mixing, mixer_f)
        carried_out = jnp.einsum('ghpn,tgn->tghp', carried, out_f, precision=lax.Precision.HIGHEST)
        carried_out = carried_out * jnp.exp(cumul).transpose(2, 0, 1)[..., None]
        direct = skip_gain.reshape(GROUPS, heads_group)[None, :, :, None] * mixer_f
        outputs = inner + carried_out + direct
        weight_end = jnp.exp(cumul[..., -1:] - cumul) * steps_here
        weighted = (mixer_f * weight_end.transpose(2, 0, 1)[..., None]).astype(jnp.bfloat16)
        weighted = lax.optimization_barrier(weighted).astype(jnp.float32)
        local_state = jnp.einsum('sghp,sgn->ghpn', weighted, in_maps.astype(jnp.float32))
        new_state = jnp.exp(cumul[..., -1])[..., None, None] * carried + local_state
        return (new_state, outputs.reshape(TOK_DEV, INNER))
    start_state = jnp.zeros((GROUPS, heads_group, P_SIZE, N), jnp.float32)
    _, mixed = lax.scan(ssm_block, start_state, jnp.arange(N_CTX, dtype=jnp.int32))
    mixed = mixed.reshape(SEQUENCE_TOKENS, INNER)
    gated = mixed * jax.nn.silu(gate_input.astype(jnp.float32))
    mean_square = lax.optimization_barrier(jnp.mean(gated * gated, axis=-1, keepdims=True))
    return (gated * lax.rsqrt(mean_square + 1e-05) * norm_gain.astype(jnp.float32)).astype(jnp.bfloat16)

def reference(queries, key_rows, value_head_rows, ssm_input, gate_input, b_matrix, c_matrix, step_size, log_decay, skip_gain, norm_gain):
    attention_out = attention_part(queries, key_rows, value_head_rows)
    mixer_out = mixer_part(ssm_input, gate_input, b_matrix, c_matrix, step_size, log_decay, skip_gain, norm_gain)
    return (attention_out, mixer_out)
```

```python
import functools

import jax
import jax.numpy as jnp
from jax import lax
from jax.experimental import pallas as pl
from jax.experimental.pallas import tpu as pltpu
from jax.sharding import PartitionSpec as P

HEAD_WIDTH = 128
STATE_HEADS = 128
P_SIZE = 64
N = 128


causal_score = -1e30


def attend_kernel(pos_ref, q_ref, kv_ref, o_ref, m_sc, l_sc, acc_sc, *, heads, width):
    key_block = pl.program_id(0)
    position = pos_ref[0]
    score_factor = width ** (-0.5)

    @pl.when(key_block == 0)
    def _init():
        m_sc[...] = jnp.full(m_sc.shape, causal_score, jnp.float32)
        l_sc[...] = jnp.zeros(l_sc.shape, jnp.float32)
        acc_sc[...] = jnp.zeros(acc_sc.shape, jnp.float32)

    def run_block(masked):
        key_portion = kv_ref[0]
        value_portion = kv_ref[1]
        rows = q_ref.shape[0]
        if masked:
            query_idx = lax.broadcasted_iota(jnp.int32, (rows, key_portion.shape[0]), 0)
            key_idx = lax.broadcasted_iota(jnp.int32, (rows, key_portion.shape[0]), 1)
            is_valid = key_idx <= query_idx
        for h in range(heads):
            query_rows = q_ref[:, h * width:(h + 1) * width]
            score_matrix = (
                lax.dot_general(
                    query_rows,
                    key_portion,
                    (((1,), (1,)), ((), ())),
                    preferred_element_type=jnp.float32,
                )
                * score_factor
            )
            if masked:
                score_matrix = jnp.where(is_valid, score_matrix, causal_score)
            run_max = m_sc[h]
            new_max = jnp.maximum(run_max, jnp.max(score_matrix, axis=-1, keepdims=True))
            weights = jnp.exp(score_matrix - new_max)
            if masked:
                weights = jnp.where(is_valid, weights, 0.0)
            correction_factor = jnp.exp(run_max - new_max)
            l_sc[h] = l_sc[h] * correction_factor + jnp.sum(weights, axis=-1, keepdims=True)
            acc_sc[h] = acc_sc[h] * correction_factor + jnp.dot(
                weights.astype(jnp.bfloat16), value_portion, preferred_element_type=jnp.float32
            )
            m_sc[h] = new_max

    @pl.when(key_block < position)
    def _full():
        run_block(False)

    @pl.when(key_block == position)
    def _diagonal():
        run_block(True)
        for h in range(heads):
            o_ref[:, h * width:(h + 1) * width] = (acc_sc[h] / l_sc[h]).astype(o_ref.dtype)


def causal_attention(position, queries, gathered_kv):
    blocks, _, tok_rows, width = gathered_kv.shape
    heads = queries.shape[1] // width
    kernel = functools.partial(attend_kernel, heads=heads, width=width)
    grid_spec = pltpu.PrefetchScalarGridSpec(
        num_scalar_prefetch=1,
        grid=(blocks,),
        in_specs=[
            pl.BlockSpec(queries.shape, lambda kb, pos: (0, 0)),
            pl.BlockSpec(
                (None, 2, tok_rows, width),
                lambda kb, pos: (jnp.minimum(kb, pos[0]), 0, 0, 0),
            ),
        ],
        out_specs=pl.BlockSpec(queries.shape, lambda kb, pos: (0, 0)),
        scratch_shapes=[
            pltpu.VMEM((heads, tok_rows, 1), jnp.float32),
            pltpu.VMEM((heads, tok_rows, 1), jnp.float32),
            pltpu.VMEM((heads, tok_rows, width), jnp.float32),
        ],
    )
    flops = 4 * queries.shape[0] * queries.shape[1] * tok_rows * blocks
    return pl.pallas_call(
        kernel,
        grid_spec=grid_spec,
        out_shape=jax.ShapeDtypeStruct(queries.shape, queries.dtype),
        compiler_params=pltpu.CompilerParams(dimension_semantics=("arbitrary",)),
        cost_estimate=pl.CostEstimate(
            flops=flops,
            transcendentals=heads * queries.shape[0] * tok_rows * blocks,
            bytes_accessed=2 * queries.size * 2 + gathered_kv.size * 2,
        ),
    )(position.reshape(1), queries, gathered_kv)


def local(
    queries,
    key_rows,
    value_head_rows,
    ssm_input,
    gate_input,
    b_matrix,
    c_matrix,
    step_size,
    log_decay,
    skip_gain,
    norm_gain,
):
    tok_rows = queries.shape[0]
    ctx_count = lax.axis_size("ctx")
    position = lax.axis_index("ctx")

    gathered_kv = lax.all_gather(jnp.stack((key_rows, value_head_rows)), "ctx")

    heads_local = step_size.shape[0]
    groups_local = b_matrix.shape[1] // N
    heads_group = heads_local // groups_local
    mixer_in = ssm_input.reshape(tok_rows, groups_local, heads_group, P_SIZE)
    in_maps = b_matrix.reshape(tok_rows, groups_local, N)
    out_maps = c_matrix.reshape(tok_rows, groups_local, N)
    steps_here = step_size.reshape(groups_local, heads_group, tok_rows)
    cumul = jnp.cumsum(log_decay.reshape(groups_local, heads_group, tok_rows), axis=-1)
    causal = jnp.tril(jnp.ones((tok_rows, tok_rows), dtype=bool))
    gram = jnp.einsum("tgn,sgn->gts", out_maps, in_maps, preferred_element_type=jnp.float32)
    spread = jnp.where(causal, cumul[..., :, None] - cumul[..., None, :], 0.0)
    mixing = jnp.where(
        causal, gram[:, None] * jnp.exp(spread) * steps_here[..., None, :], 0.0
    ).astype(jnp.bfloat16)
    inner = jnp.einsum("ghts,sghp->tghp", mixing, mixer_in, preferred_element_type=jnp.float32)
    weight_end = jnp.exp(cumul[..., -1:] - cumul) * steps_here
    weighted = (mixer_in * weight_end.transpose(2, 0, 1)[..., None]).astype(jnp.bfloat16)
    local_state = jnp.einsum(
        "sghp,sgn->ghpn", weighted, in_maps, preferred_element_type=jnp.float32
    )
    block_log_decay = cumul[..., -1]

    states = lax.all_gather(local_state.astype(jnp.bfloat16), "ctx")
    log_decays = lax.all_gather(block_log_decay, "ctx")
    source = jnp.arange(ctx_count, dtype=jnp.int32)
    between = (source[None, :] > source[:, None]) & (source[None, :] < position)
    span_decay = jnp.sum(
        jnp.where(between[:, :, None, None], log_decays[None, :], 0.0), axis=1
    )
    state_weight = jnp.where(
        (source < position)[:, None, None], jnp.exp(span_decay), 0.0
    )
    incoming = jnp.sum(
        state_weight[..., None, None] * states.astype(jnp.float32), axis=0
    )

    attention_out = causal_attention(position, queries, gathered_kv)

    carried_out = jnp.einsum(
        "ghpn,tgn->tghp", incoming, out_maps.astype(jnp.float32), precision=lax.Precision.HIGHEST
    )
    carried_out = carried_out * jnp.exp(cumul).transpose(2, 0, 1)[..., None]
    direct = skip_gain.reshape(groups_local, heads_group)[None, :, :, None] * mixer_in.astype(
        jnp.float32
    )
    outputs = (inner + carried_out + direct).reshape(tok_rows, -1)
    gated = outputs * jax.nn.silu(gate_input.astype(jnp.float32))
    square_parts = lax.all_gather(jnp.sum(gated * gated, axis=-1), "tp")
    square_total = jnp.sum(square_parts, axis=0)
    scaling = lax.rsqrt(square_total / (STATE_HEADS * P_SIZE) + 1e-05)
    mixer_out = (gated * scaling[:, None] * norm_gain.astype(jnp.float32)).astype(jnp.bfloat16)
    return (attention_out, mixer_out)


def solution(mesh):
    placed = (
        P("ctx", "tp"),
        P("ctx", "tp"),
        P("ctx", "tp"),
        P("ctx", "tp"),
        P("ctx", "tp"),
        P("ctx", "tp"),
        P("ctx", "tp"),
        P("tp", "ctx"),
        P("tp", "ctx"),
        P("tp"),
        P("tp"),
    )
    return jax.shard_map(
        local,
        mesh=mesh,
        in_specs=placed,
        out_specs=(P("ctx", "tp"), P("ctx", "tp")),
        check_vma=False,
    )
```

```python
import functools

import jax
import jax.numpy as jnp
from jax import lax
from jax.experimental import pallas as pl
from jax.experimental.pallas import tpu as pltpu
from jax.sharding import PartitionSpec as P

HEAD_WIDTH = 128
STATE_HEADS = 128
P_SIZE = 64
N = 128


causal_score = -1e30


def attend_kernel(pos_ref, q_ref, kv_ref, o_ref, m_sc, l_sc, acc_sc, *, heads, width):
    key_block = pl.program_id(0)
    position = pos_ref[0]
    score_factor = width ** (-0.5)

    @pl.when(key_block == 0)
    def _init():
        m_sc[...] = jnp.full(m_sc.shape, causal_score, jnp.float32)
        l_sc[...] = jnp.zeros(l_sc.shape, jnp.float32)
        acc_sc[...] = jnp.zeros(acc_sc.shape, jnp.float32)

    def run_block(masked):
        key_portion = kv_ref[0]
        value_portion = kv_ref[1]
        rows = q_ref.shape[0]
        if masked:
            query_idx = lax.broadcasted_iota(jnp.int32, (rows, key_portion.shape[0]), 0)
            key_idx = lax.broadcasted_iota(jnp.int32, (rows, key_portion.shape[0]), 1)
            is_valid = key_idx <= query_idx
        for h in range(heads):
            query_rows = q_ref[:, h * width:(h + 1) * width]
            score_matrix = (
                lax.dot_general(
                    query_rows,
                    key_portion,
                    (((1,), (1,)), ((), ())),
                    preferred_element_type=jnp.float32,
                )
                * score_factor
            )
            if masked:
                score_matrix = jnp.where(is_valid, score_matrix, causal_score)
            run_max = m_sc[h]
            new_max = jnp.maximum(run_max, jnp.max(score_matrix, axis=-1, keepdims=True))
            weights = jnp.exp(score_matrix - new_max)
            if masked:
                weights = jnp.where(is_valid, weights, 0.0)
            correction_factor = jnp.exp(run_max - new_max)
            l_sc[h] = l_sc[h] * correction_factor + jnp.sum(weights, axis=-1, keepdims=True)
            acc_sc[h] = acc_sc[h] * correction_factor + jnp.dot(
                weights.astype(jnp.bfloat16), value_portion, preferred_element_type=jnp.float32
            )
            m_sc[h] = new_max

    @pl.when(key_block < position)
    def _full():
        run_block(False)

    @pl.when(key_block == position)
    def _diagonal():
        run_block(True)
        for h in range(heads):
            o_ref[:, h * width:(h + 1) * width] = (acc_sc[h] / l_sc[h]).astype(o_ref.dtype)


def causal_attention(position, queries, gathered_kv):
    blocks, _, tok_rows, width = gathered_kv.shape
    heads = queries.shape[1] // width
    kernel = functools.partial(attend_kernel, heads=heads, width=width)
    grid_spec = pltpu.PrefetchScalarGridSpec(
        num_scalar_prefetch=1,
        grid=(blocks,),
        in_specs=[
            pl.BlockSpec(queries.shape, lambda kb, pos: (0, 0)),
            pl.BlockSpec(
                (None, 2, tok_rows, width),
                lambda kb, pos: (jnp.minimum(kb, pos[0]), 0, 0, 0),
            ),
        ],
        out_specs=pl.BlockSpec(queries.shape, lambda kb, pos: (0, 0)),
        scratch_shapes=[
            pltpu.VMEM((heads, tok_rows, 1), jnp.float32),
            pltpu.VMEM((heads, tok_rows, 1), jnp.float32),
            pltpu.VMEM((heads, tok_rows, width), jnp.float32),
        ],
    )
    flops = 4 * queries.shape[0] * queries.shape[1] * tok_rows * blocks
    return pl.pallas_call(
        kernel,
        grid_spec=grid_spec,
        out_shape=jax.ShapeDtypeStruct(queries.shape, queries.dtype),
        compiler_params=pltpu.CompilerParams(dimension_semantics=("arbitrary",)),
        cost_estimate=pl.CostEstimate(
            flops=flops,
            transcendentals=heads * queries.shape[0] * tok_rows * blocks,
            bytes_accessed=2 * queries.size * 2 + gathered_kv.size * 2,
        ),
    )(position.reshape(1), queries, gathered_kv)


def shifted(block, axis, distance):
    devices = range(lax.axis_size(axis))
    route = [(i - distance, i) for i in devices if i - distance in devices]
    return lax.ppermute(block, axis, route)


def summed_over(part, axis):
    count = lax.axis_size(axis)
    total = part
    for distance in range(1, count):
        route = [(i, (i + distance) % count) for i in range(count)]
        total = total + lax.ppermute(part, axis, route)
    return total


def carried_scan(local_state, block_log_decay, position, ctx_count):
    sent = local_state.astype(jnp.bfloat16)
    one_back_state = shifted(sent, "ctx", 1).astype(jnp.float32)
    one_back_decay = shifted(block_log_decay, "ctx", 1)
    two_back_state = shifted(sent, "ctx", 2).astype(jnp.float32)
    two_back_decay = shifted(block_log_decay, "ctx", 2)
    state = jnp.exp(one_back_decay)[..., None, None] * two_back_state + one_back_state
    log_span = one_back_decay + two_back_decay
    distance = 2
    while distance < ctx_count:
        earlier_state = shifted(state.astype(jnp.bfloat16), "ctx", distance).astype(jnp.float32)
        earlier_span = shifted(log_span, "ctx", distance)
        state = jnp.exp(log_span)[..., None, None] * earlier_state + state
        log_span = log_span + earlier_span
        distance *= 2
    return state


def local(
    queries,
    key_rows,
    value_head_rows,
    ssm_input,
    gate_input,
    b_matrix,
    c_matrix,
    step_size,
    log_decay,
    skip_gain,
    norm_gain,
):
    tok_rows = queries.shape[0]
    ctx_count = lax.axis_size("ctx")
    position = lax.axis_index("ctx")

    gathered_kv = lax.all_gather(jnp.stack((key_rows, value_head_rows)), "ctx")

    heads_local = step_size.shape[0]
    groups_local = b_matrix.shape[1] // N
    heads_group = heads_local // groups_local
    mixer_in = ssm_input.reshape(tok_rows, groups_local, heads_group, P_SIZE)
    in_maps = b_matrix.reshape(tok_rows, groups_local, N)
    out_maps = c_matrix.reshape(tok_rows, groups_local, N)
    steps_here = step_size.reshape(groups_local, heads_group, tok_rows)
    cumul = jnp.cumsum(log_decay.reshape(groups_local, heads_group, tok_rows), axis=-1)
    causal = jnp.tril(jnp.ones((tok_rows, tok_rows), dtype=bool))
    gram = jnp.einsum("tgn,sgn->gts", out_maps, in_maps, preferred_element_type=jnp.float32)
    spread = jnp.where(causal, cumul[..., :, None] - cumul[..., None, :], 0.0)
    mixing = jnp.where(
        causal, gram[:, None] * jnp.exp(spread) * steps_here[..., None, :], 0.0
    ).astype(jnp.bfloat16)
    inner = jnp.einsum("ghts,sghp->tghp", mixing, mixer_in, preferred_element_type=jnp.float32)
    weight_end = jnp.exp(cumul[..., -1:] - cumul) * steps_here
    weighted = (mixer_in * weight_end.transpose(2, 0, 1)[..., None]).astype(jnp.bfloat16)
    local_state = jnp.einsum(
        "sghp,sgn->ghpn", weighted, in_maps, preferred_element_type=jnp.float32
    )
    block_log_decay = cumul[..., -1]

    incoming = carried_scan(local_state, block_log_decay, position, ctx_count)

    attention_out = causal_attention(position, queries, gathered_kv)

    carried_out = jnp.einsum(
        "ghpn,tgn->tghp", incoming, out_maps.astype(jnp.float32), precision=lax.Precision.HIGHEST
    )
    carried_out = carried_out * jnp.exp(cumul).transpose(2, 0, 1)[..., None]
    direct = skip_gain.reshape(groups_local, heads_group)[None, :, :, None] * mixer_in.astype(
        jnp.float32
    )
    outputs = (inner + carried_out + direct).reshape(tok_rows, -1)
    gated = outputs * jax.nn.silu(gate_input.astype(jnp.float32))
    square_total = summed_over(jnp.sum(gated * gated, axis=-1), "tp")
    scaling = lax.rsqrt(square_total / (STATE_HEADS * P_SIZE) + 1e-05)
    mixer_out = (gated * scaling[:, None] * norm_gain.astype(jnp.float32)).astype(jnp.bfloat16)
    return (attention_out, mixer_out)


def solution(mesh):
    placed = (
        P("ctx", "tp"),
        P("ctx", "tp"),
        P("ctx", "tp"),
        P("ctx", "tp"),
        P("ctx", "tp"),
        P("ctx", "tp"),
        P("ctx", "tp"),
        P("tp", "ctx"),
        P("tp", "ctx"),
        P("tp"),
        P("tp"),
    )
    return jax.shard_map(
        local,
        mesh=mesh,
        in_specs=placed,
        out_specs=(P("ctx", "tp"), P("ctx", "tp")),
        check_vma=False,
    )
```

```python
import functools

import jax
import jax.numpy as jnp
from jax import lax
from jax.experimental import pallas as pl
from jax.experimental.pallas import tpu as pltpu
from jax.sharding import PartitionSpec as P

HEAD_WIDTH = 128
STATE_HEADS = 128
P_SIZE = 64
N = 128


causal_score = -1e30


def attend_kernel(pos_ref, qt_ref, kv_ref, o_ref, p_sc, m_sc, l_sc, c_sc, acc_sc, *, tok, width, chunk):
    position = pos_ref[0]
    score_factor = width ** (-0.5)
    rows = qt_ref.shape[1]
    block_rows = kv_ref.shape[2]
    m_sc[...] = jnp.full(m_sc.shape, causal_score, jnp.float32)
    l_sc[...] = jnp.zeros(l_sc.shape, jnp.float32)
    acc_sc[...] = jnp.zeros(acc_sc.shape, jnp.float32)

    def run_block(kb, masked):
        key_portion = kv_ref[kb, 0]
        for c in range(rows // chunk):
            r0 = c * chunk
            score_t = jnp.dot(key_portion, qt_ref[:, r0:r0 + chunk],
                              preferred_element_type=jnp.float32) * score_factor
            if masked:
                key_idx = lax.broadcasted_iota(jnp.int32, (block_rows, chunk), 0)
                query_idx = (r0 % tok) + lax.broadcasted_iota(jnp.int32, (block_rows, chunk), 1)
                is_valid = key_idx <= query_idx
                score_t = jnp.where(is_valid, score_t, causal_score)
            run_max = m_sc[:, r0:r0 + chunk]
            new_max = jnp.maximum(run_max, jnp.max(score_t, axis=0, keepdims=True))
            weights = jnp.exp(score_t - new_max)
            if masked:
                weights = jnp.where(is_valid, weights, 0.0)
            correction_factor = jnp.exp(run_max - new_max)
            l_sc[:, r0:r0 + chunk] = l_sc[:, r0:r0 + chunk] * correction_factor + jnp.sum(weights, axis=0, keepdims=True)
            m_sc[:, r0:r0 + chunk] = new_max
            c_sc[:, r0:r0 + chunk] = correction_factor
            p_sc[:, r0:r0 + chunk] = weights.astype(jnp.bfloat16)
        acc_sc[...] = acc_sc[...] * c_sc[...] + lax.dot_general(kv_ref[kb, 1], p_sc[...], (((0,), (0,)), ((), ())), preferred_element_type=jnp.float32)

    def body(kb, carry):
        run_block(kb, False)
        return carry
    lax.fori_loop(0, position, body, 0)
    run_block(position, True)
    o_ref[...] = (acc_sc[...] / l_sc[...]).astype(o_ref.dtype)


def causal_attention(position, queries, gathered_kv, chunk=256):
    blocks, _, tok_rows, width = gathered_kv.shape
    heads = queries.shape[1] // width
    rows = heads * tok_rows
    queries_t = queries.reshape(tok_rows, heads, width).transpose(2, 1, 0).reshape(width, rows)
    kernel = functools.partial(attend_kernel, tok=tok_rows, width=width, chunk=chunk)
    out_t = pl.pallas_call(
        kernel,
        in_specs=[pl.BlockSpec(memory_space=pltpu.SMEM)] + [pl.BlockSpec(memory_space=pltpu.VMEM)] * 2,
        out_specs=pl.BlockSpec(memory_space=pltpu.VMEM),
        out_shape=jax.ShapeDtypeStruct((width, rows), queries.dtype),
        scratch_shapes=[
            pltpu.VMEM((tok_rows, rows), jnp.bfloat16),
            pltpu.VMEM((1, rows), jnp.float32),
            pltpu.VMEM((1, rows), jnp.float32),
            pltpu.VMEM((1, rows), jnp.float32),
            pltpu.VMEM((width, rows), jnp.float32),
        ],
    )(position.reshape(1), queries_t, gathered_kv)
    return out_t.reshape(width, heads, tok_rows).transpose(2, 1, 0).reshape(tok_rows, heads * width)


def shifted(block, axis, distance):
    devices = range(lax.axis_size(axis))
    route = [(i - distance, i) for i in devices if i - distance in devices]
    return lax.ppermute(block, axis, route)


def summed_over(part, axis):
    count = lax.axis_size(axis)
    total = part
    for distance in range(1, count):
        route = [(i, (i + distance) % count) for i in range(count)]
        total = total + lax.ppermute(part, axis, route)
    return total


def carried_scan(local_state, block_log_decay, position, ctx_count):
    sent = local_state.astype(jnp.bfloat16)
    one_back_state = shifted(sent, "ctx", 1).astype(jnp.float32)
    one_back_decay = shifted(block_log_decay, "ctx", 1)
    two_back_state = shifted(sent, "ctx", 2).astype(jnp.float32)
    two_back_decay = shifted(block_log_decay, "ctx", 2)
    state = jnp.exp(one_back_decay)[..., None, None] * two_back_state + one_back_state
    log_span = one_back_decay + two_back_decay
    distance = 2
    while distance < ctx_count:
        earlier_state = shifted(state.astype(jnp.bfloat16), "ctx", distance).astype(jnp.float32)
        earlier_span = shifted(log_span, "ctx", distance)
        state = jnp.exp(log_span)[..., None, None] * earlier_state + state
        log_span = log_span + earlier_span
        distance *= 2
    return state


def local(
    queries,
    key_rows,
    value_head_rows,
    ssm_input,
    gate_input,
    b_matrix,
    c_matrix,
    step_size,
    log_decay,
    skip_gain,
    norm_gain,
):
    tok_rows = queries.shape[0]
    ctx_count = lax.axis_size("ctx")
    position = lax.axis_index("ctx")

    gathered_kv = lax.all_gather(jnp.stack((key_rows, value_head_rows)), "ctx")

    heads_local = step_size.shape[0]
    groups_local = b_matrix.shape[1] // N
    heads_group = heads_local // groups_local
    mixer_in = ssm_input.reshape(tok_rows, groups_local, heads_group, P_SIZE)
    in_maps = b_matrix.reshape(tok_rows, groups_local, N)
    out_maps = c_matrix.reshape(tok_rows, groups_local, N)
    steps_here = step_size.reshape(groups_local, heads_group, tok_rows)
    cumul = jnp.cumsum(log_decay.reshape(groups_local, heads_group, tok_rows), axis=-1)
    causal = jnp.tril(jnp.ones((tok_rows, tok_rows), dtype=bool))
    gram = jnp.einsum("tgn,sgn->gts", out_maps, in_maps, preferred_element_type=jnp.float32)
    spread = jnp.where(causal, cumul[..., :, None] - cumul[..., None, :], 0.0)
    mixing = jnp.where(
        causal, gram[:, None] * jnp.exp(spread) * steps_here[..., None, :], 0.0
    ).astype(jnp.bfloat16)
    inner = jnp.einsum("ghts,sghp->tghp", mixing, mixer_in, preferred_element_type=jnp.float32)
    weight_end = jnp.exp(cumul[..., -1:] - cumul) * steps_here
    weighted = (mixer_in * weight_end.transpose(2, 0, 1)[..., None]).astype(jnp.bfloat16)
    local_state = jnp.einsum(
        "sghp,sgn->ghpn", weighted, in_maps, preferred_element_type=jnp.float32
    )
    block_log_decay = cumul[..., -1]

    incoming = carried_scan(local_state, block_log_decay, position, ctx_count)

    attention_out = causal_attention(position, queries, gathered_kv)

    carried_out = jnp.einsum(
        "ghpn,tgn->tghp", incoming, out_maps.astype(jnp.float32), precision=lax.Precision.HIGHEST
    )
    carried_out = carried_out * jnp.exp(cumul).transpose(2, 0, 1)[..., None]
    direct = skip_gain.reshape(groups_local, heads_group)[None, :, :, None] * mixer_in.astype(
        jnp.float32
    )
    outputs = (inner + carried_out + direct).reshape(tok_rows, -1)
    gated = outputs * jax.nn.silu(gate_input.astype(jnp.float32))
    square_total = summed_over(jnp.sum(gated * gated, axis=-1), "tp")
    scaling = lax.rsqrt(square_total / (STATE_HEADS * P_SIZE) + 1e-05)
    mixer_out = (gated * scaling[:, None] * norm_gain.astype(jnp.float32)).astype(jnp.bfloat16)
    return (attention_out, mixer_out)


def solution(mesh):
    placed = (
        P("ctx", "tp"),
        P("ctx", "tp"),
        P("ctx", "tp"),
        P("ctx", "tp"),
        P("ctx", "tp"),
        P("ctx", "tp"),
        P("ctx", "tp"),
        P("tp", "ctx"),
        P("tp", "ctx"),
        P("tp"),
        P("tp"),
    )
    return jax.shard_map(
        local,
        mesh=mesh,
        in_specs=placed,
        out_specs=(P("ctx", "tp"), P("ctx", "tp")),
        check_vma=False,
    )
```

```python
import functools

import jax
import jax.numpy as jnp
from jax import lax
from jax.experimental import pallas as pl
from jax.experimental.pallas import tpu as pltpu
from jax.sharding import PartitionSpec as P

HEAD_WIDTH = 128
STATE_HEADS = 128
P_SIZE = 64
N = 128


causal_score = -1e30


def attend_kernel(pos_ref, qt_ref, kv_ref, o_ref, p_sc, m_sc, l_sc, c_sc, acc_sc, *, tok, width, chunk):
    position = pos_ref[0]
    score_factor = width ** (-0.5)
    rows = qt_ref.shape[1]
    block_rows = kv_ref.shape[2]
    m_sc[...] = jnp.full(m_sc.shape, causal_score, jnp.float32)
    l_sc[...] = jnp.zeros(l_sc.shape, jnp.float32)
    acc_sc[...] = jnp.zeros(acc_sc.shape, jnp.float32)

    def run_block(kb, masked):
        key_portion = kv_ref[kb, 0]
        for c in range(rows // chunk):
            r0 = c * chunk
            score_t = jnp.dot(key_portion, qt_ref[:, r0:r0 + chunk],
                              preferred_element_type=jnp.float32) * score_factor
            if masked:
                key_idx = lax.broadcasted_iota(jnp.int32, (block_rows, chunk), 0)
                query_idx = (r0 % tok) + lax.broadcasted_iota(jnp.int32, (block_rows, chunk), 1)
                is_valid = key_idx <= query_idx
                score_t = jnp.where(is_valid, score_t, causal_score)
            run_max = m_sc[:, r0:r0 + chunk]
            new_max = jnp.maximum(run_max, jnp.max(score_t, axis=0, keepdims=True))
            weights = jnp.exp(score_t - new_max)
            if masked:
                weights = jnp.where(is_valid, weights, 0.0)
            correction_factor = jnp.exp(run_max - new_max)
            l_sc[:, r0:r0 + chunk] = l_sc[:, r0:r0 + chunk] * correction_factor + jnp.sum(weights, axis=0, keepdims=True)
            m_sc[:, r0:r0 + chunk] = new_max
            c_sc[:, r0:r0 + chunk] = correction_factor
            p_sc[:, r0:r0 + chunk] = weights.astype(jnp.bfloat16)
        acc_sc[...] = acc_sc[...] * c_sc[...] + lax.dot_general(kv_ref[kb, 1], p_sc[...], (((0,), (0,)), ((), ())), preferred_element_type=jnp.float32)

    def body(kb, carry):
        run_block(kb, False)
        return carry
    lax.fori_loop(0, position, body, 0)
    run_block(position, True)
    o_ref[...] = (acc_sc[...] / l_sc[...]).astype(o_ref.dtype)


def causal_attention(position, queries, gathered_kv, chunk=256):
    blocks, _, tok_rows, width = gathered_kv.shape
    heads = queries.shape[1] // width
    rows = heads * tok_rows
    queries_t = queries.reshape(tok_rows, heads, width).transpose(2, 1, 0).reshape(width, rows)
    kernel = functools.partial(attend_kernel, tok=tok_rows, width=width, chunk=chunk)
    out_t = pl.pallas_call(
        kernel,
        in_specs=[pl.BlockSpec(memory_space=pltpu.SMEM)] + [pl.BlockSpec(memory_space=pltpu.VMEM)] * 2,
        out_specs=pl.BlockSpec(memory_space=pltpu.VMEM),
        out_shape=jax.ShapeDtypeStruct((width, rows), queries.dtype),
        scratch_shapes=[
            pltpu.VMEM((tok_rows, rows), jnp.bfloat16),
            pltpu.VMEM((1, rows), jnp.float32),
            pltpu.VMEM((1, rows), jnp.float32),
            pltpu.VMEM((1, rows), jnp.float32),
            pltpu.VMEM((width, rows), jnp.float32),
        ],
    )(position.reshape(1), queries_t, gathered_kv)
    return out_t.reshape(width, heads, tok_rows).transpose(2, 1, 0).reshape(tok_rows, heads * width)


def shifted(block, axis, distance):
    devices = range(lax.axis_size(axis))
    route = [(i - distance, i) for i in devices if i - distance in devices]
    return lax.ppermute(block, axis, route)


def summed_over(part, axis):
    count = lax.axis_size(axis)
    total = part
    distance = 1
    while distance < count:
        route = [(i, i ^ distance) for i in range(count)]
        total = total + lax.ppermute(total, axis, route)
        distance *= 2
    return total


def packed(state, log_span):
    heads = log_span.shape[-1]
    lanes = state.shape[-1]
    rows = state.astype(jnp.bfloat16).reshape(state.shape[0], -1, lanes)
    high = lax.reduce_precision(log_span, exponent_bits=8, mantissa_bits=7)
    rest = log_span - high
    middle = lax.reduce_precision(rest, exponent_bits=8, mantissa_bits=7)
    low = rest - middle
    parts = jnp.stack((high, middle, low), axis=1).astype(jnp.bfloat16)
    tail = jnp.pad(parts, ((0, 0), (0, 16 - parts.shape[1]), (0, lanes - heads)))
    return jnp.concatenate((rows, tail), axis=1)


def unpacked(block, state_shape):
    heads = state_shape[1]
    body_rows = block.shape[1] - 16
    state = block[:, :body_rows].reshape(state_shape).astype(jnp.float32)
    parts = block[:, body_rows:body_rows + 3, :heads].astype(jnp.float32)
    return state, (parts[:, 0] + parts[:, 1]) + parts[:, 2]


def carried_scan(local_state, block_log_decay, position, ctx_count):
    sent = packed(local_state, block_log_decay)
    one_back_state, one_back_decay = unpacked(shifted(sent, "ctx", 1), local_state.shape)
    two_back_state, two_back_decay = unpacked(shifted(sent, "ctx", 2), local_state.shape)
    state = jnp.exp(one_back_decay)[..., None, None] * two_back_state + one_back_state
    log_span = one_back_decay + two_back_decay
    distance = 2
    while distance < ctx_count:
        earlier_state, earlier_span = unpacked(
            shifted(packed(state, log_span), "ctx", distance), local_state.shape
        )
        state = jnp.exp(log_span)[..., None, None] * earlier_state + state
        log_span = log_span + earlier_span
        distance *= 2
    return state


def local(
    queries,
    key_rows,
    value_head_rows,
    ssm_input,
    gate_input,
    b_matrix,
    c_matrix,
    step_size,
    log_decay,
    skip_gain,
    norm_gain,
):
    tok_rows = queries.shape[0]
    ctx_count = lax.axis_size("ctx")
    position = lax.axis_index("ctx")

    gathered_kv = lax.all_gather(jnp.stack((key_rows, value_head_rows)), "ctx")

    heads_local = step_size.shape[0]
    groups_local = b_matrix.shape[1] // N
    heads_group = heads_local // groups_local
    mixer_in = ssm_input.reshape(tok_rows, groups_local, heads_group, P_SIZE)
    in_maps = b_matrix.reshape(tok_rows, groups_local, N)
    out_maps = c_matrix.reshape(tok_rows, groups_local, N)
    steps_here = step_size.reshape(groups_local, heads_group, tok_rows)
    cumul = jnp.cumsum(log_decay.reshape(groups_local, heads_group, tok_rows), axis=-1)
    causal = jnp.tril(jnp.ones((tok_rows, tok_rows), dtype=bool))
    gram = jnp.einsum("tgn,sgn->gts", out_maps, in_maps, preferred_element_type=jnp.float32)
    spread = jnp.where(causal, cumul[..., :, None] - cumul[..., None, :], 0.0)
    mixing = jnp.where(
        causal, gram[:, None] * jnp.exp(spread) * steps_here[..., None, :], 0.0
    ).astype(jnp.bfloat16)
    inner = jnp.einsum("ghts,sghp->tghp", mixing, mixer_in, preferred_element_type=jnp.float32)
    weight_end = jnp.exp(cumul[..., -1:] - cumul) * steps_here
    weighted = (mixer_in * weight_end.transpose(2, 0, 1)[..., None]).astype(jnp.bfloat16)
    local_state = jnp.einsum(
        "sghp,sgn->ghpn", weighted, in_maps, preferred_element_type=jnp.float32
    )
    block_log_decay = cumul[..., -1]

    incoming = carried_scan(local_state, block_log_decay, position, ctx_count)

    attention_out = causal_attention(position, queries, gathered_kv)

    carried_out = jnp.einsum(
        "ghpn,tgn->tghp", incoming, out_maps.astype(jnp.float32), precision=lax.Precision.HIGHEST
    )
    carried_out = carried_out * jnp.exp(cumul).transpose(2, 0, 1)[..., None]
    direct = skip_gain.reshape(groups_local, heads_group)[None, :, :, None] * mixer_in.astype(
        jnp.float32
    )
    outputs = (inner + carried_out + direct).reshape(tok_rows, -1)
    gated = outputs * jax.nn.silu(gate_input.astype(jnp.float32))
    square_total = summed_over(jnp.sum(gated * gated, axis=-1), "tp")
    scaling = lax.rsqrt(square_total / (STATE_HEADS * P_SIZE) + 1e-05)
    mixer_out = (gated * scaling[:, None] * norm_gain.astype(jnp.float32)).astype(jnp.bfloat16)
    return (attention_out, mixer_out)


def solution(mesh):
    placed = (
        P("ctx", "tp"),
        P("ctx", "tp"),
        P("ctx", "tp"),
        P("ctx", "tp"),
        P("ctx", "tp"),
        P("ctx", "tp"),
        P("ctx", "tp"),
        P("tp", "ctx"),
        P("tp", "ctx"),
        P("tp"),
        P("tp"),
    )
    return jax.shard_map(
        local,
        mesh=mesh,
        in_specs=placed,
        out_specs=(P("ctx", "tp"), P("ctx", "tp")),
        check_vma=False,
    )
```

```python
import functools

import jax
import jax.numpy as jnp
from jax import lax
from jax.experimental import pallas as pl
from jax.experimental.pallas import tpu as pltpu
from jax.sharding import PartitionSpec as P

HEAD_WIDTH = 128
STATE_HEADS = 128
P_SIZE = 64
N = 128


causal_score = -1e30
CTX = ("chip", "core")


def attend_kernel(pos_ref, qt_ref, same_ref, other_ref, o_ref, p_sc, m_sc, l_sc, c_sc, acc_sc, *, tok, width, chunk):
    position = pos_ref[0]
    core = lax.rem(position, 2)
    score_factor = width ** (-0.5)
    rows = qt_ref.shape[1]
    block_rows = same_ref.shape[2]
    m_sc[...] = jnp.full(m_sc.shape, causal_score, jnp.float32)
    l_sc[...] = jnp.zeros(l_sc.shape, jnp.float32)
    acc_sc[...] = jnp.zeros(acc_sc.shape, jnp.float32)

    def run_block(kb, masked):
        chip = kb // 2
        from_same = lax.rem(kb, 2) == core
        key_portion = jnp.where(from_same, same_ref[chip, 0], other_ref[chip, 0])
        value_portion = jnp.where(from_same, same_ref[chip, 1], other_ref[chip, 1])
        for c in range(rows // chunk):
            r0 = c * chunk
            score_t = jnp.dot(key_portion, qt_ref[:, r0:r0 + chunk],
                              preferred_element_type=jnp.float32) * score_factor
            if masked:
                key_idx = lax.broadcasted_iota(jnp.int32, (block_rows, chunk), 0)
                query_idx = (r0 % tok) + lax.broadcasted_iota(jnp.int32, (block_rows, chunk), 1)
                is_valid = key_idx <= query_idx
                score_t = jnp.where(is_valid, score_t, causal_score)
            run_max = m_sc[:, r0:r0 + chunk]
            new_max = jnp.maximum(run_max, jnp.max(score_t, axis=0, keepdims=True))
            weights = jnp.exp(score_t - new_max)
            if masked:
                weights = jnp.where(is_valid, weights, 0.0)
            correction_factor = jnp.exp(run_max - new_max)
            l_sc[:, r0:r0 + chunk] = l_sc[:, r0:r0 + chunk] * correction_factor + jnp.sum(weights, axis=0, keepdims=True)
            m_sc[:, r0:r0 + chunk] = new_max
            c_sc[:, r0:r0 + chunk] = correction_factor
            p_sc[:, r0:r0 + chunk] = weights.astype(jnp.bfloat16)
        acc_sc[...] = acc_sc[...] * c_sc[...] + lax.dot_general(value_portion, p_sc[...], (((0,), (0,)), ((), ())), preferred_element_type=jnp.float32)

    def body(kb, carry):
        run_block(kb, False)
        return carry
    lax.fori_loop(0, position, body, 0)
    run_block(position, True)
    o_ref[...] = (acc_sc[...] / l_sc[...]).astype(o_ref.dtype)


def causal_attention(position, queries, same_core_kv, other_core_kv, chunk=256):
    _, _, tok_rows, width = same_core_kv.shape
    heads = queries.shape[1] // width
    rows = heads * tok_rows
    queries_t = queries.reshape(tok_rows, heads, width).transpose(2, 1, 0).reshape(width, rows)
    kernel = functools.partial(attend_kernel, tok=tok_rows, width=width, chunk=chunk)
    out_t = pl.pallas_call(
        kernel,
        in_specs=[pl.BlockSpec(memory_space=pltpu.SMEM)] + [pl.BlockSpec(memory_space=pltpu.VMEM)] * 3,
        out_specs=pl.BlockSpec(memory_space=pltpu.VMEM),
        out_shape=jax.ShapeDtypeStruct((width, rows), queries.dtype),
        scratch_shapes=[
            pltpu.VMEM((tok_rows, rows), jnp.bfloat16),
            pltpu.VMEM((1, rows), jnp.float32),
            pltpu.VMEM((1, rows), jnp.float32),
            pltpu.VMEM((1, rows), jnp.float32),
            pltpu.VMEM((width, rows), jnp.float32),
        ],
    )(position.reshape(1), queries_t, same_core_kv, other_core_kv)
    return out_t.reshape(width, heads, tok_rows).transpose(2, 1, 0).reshape(tok_rows, heads * width)


def shifted(block, axis, distance):
    devices = range(lax.axis_size(axis))
    route = [(i - distance, i) for i in devices if i - distance in devices]
    return lax.ppermute(block, axis, route)


def summed_over(part, axis):
    count = lax.axis_size(axis)
    total = part
    distance = 1
    while distance < count:
        route = [(i, i ^ distance) for i in range(count)]
        total = total + lax.ppermute(total, axis, route)
        distance *= 2
    return total


def packed(state, log_span):
    heads = log_span.shape[-1]
    lanes = state.shape[-1]
    rows = state.astype(jnp.bfloat16).reshape(state.shape[0], -1, lanes)
    high = lax.reduce_precision(log_span, exponent_bits=8, mantissa_bits=7)
    rest = log_span - high
    middle = lax.reduce_precision(rest, exponent_bits=8, mantissa_bits=7)
    low = rest - middle
    parts = jnp.stack((high, middle, low), axis=1).astype(jnp.bfloat16)
    tail = jnp.pad(parts, ((0, 0), (0, 16 - parts.shape[1]), (0, lanes - heads)))
    return jnp.concatenate((rows, tail), axis=1)


def unpacked(block, state_shape):
    heads = state_shape[1]
    body_rows = block.shape[1] - 16
    state = block[:, :body_rows].reshape(state_shape).astype(jnp.float32)
    parts = block[:, body_rows:body_rows + 3, :heads].astype(jnp.float32)
    return state, (parts[:, 0] + parts[:, 1]) + parts[:, 2]


def carried_scan(local_state, block_log_decay, position, ctx_count):
    sent = packed(local_state, block_log_decay)
    one_back_state, one_back_decay = unpacked(shifted(sent, CTX, 1), local_state.shape)
    two_back_state, two_back_decay = unpacked(shifted(sent, CTX, 2), local_state.shape)
    state = jnp.exp(one_back_decay)[..., None, None] * two_back_state + one_back_state
    log_span = one_back_decay + two_back_decay
    distance = 2
    while distance < ctx_count:
        earlier_state, earlier_span = unpacked(
            shifted(packed(state, log_span), CTX, distance), local_state.shape
        )
        state = jnp.exp(log_span)[..., None, None] * earlier_state + state
        log_span = log_span + earlier_span
        distance *= 2
    return state


def local(
    queries,
    key_rows,
    value_head_rows,
    ssm_input,
    gate_input,
    b_matrix,
    c_matrix,
    step_size,
    log_decay,
    skip_gain,
    norm_gain,
):
    tok_rows = queries.shape[0]
    ctx_count = lax.axis_size(("chip", "core"))
    position = lax.axis_index(("chip", "core"))

    same_core_kv = lax.all_gather(jnp.stack((key_rows, value_head_rows)), "chip")
    other_core_kv = lax.ppermute(same_core_kv, "core", [(0, 1), (1, 0)])

    heads_local = step_size.shape[0]
    groups_local = b_matrix.shape[1] // N
    heads_group = heads_local // groups_local
    mixer_in = ssm_input.reshape(tok_rows, groups_local, heads_group, P_SIZE)
    in_maps = b_matrix.reshape(tok_rows, groups_local, N)
    out_maps = c_matrix.reshape(tok_rows, groups_local, N)
    steps_here = step_size.reshape(groups_local, heads_group, tok_rows)
    cumul = jnp.cumsum(log_decay.reshape(groups_local, heads_group, tok_rows), axis=-1)
    causal = jnp.tril(jnp.ones((tok_rows, tok_rows), dtype=bool))
    gram = jnp.einsum("tgn,sgn->gts", out_maps, in_maps, preferred_element_type=jnp.float32)
    spread = jnp.where(causal, cumul[..., :, None] - cumul[..., None, :], 0.0)
    mixing = jnp.where(
        causal, gram[:, None] * jnp.exp(spread) * steps_here[..., None, :], 0.0
    ).astype(jnp.bfloat16)
    inner = jnp.einsum("ghts,sghp->tghp", mixing, mixer_in, preferred_element_type=jnp.float32)
    weight_end = jnp.exp(cumul[..., -1:] - cumul) * steps_here
    weighted = (mixer_in * weight_end.transpose(2, 0, 1)[..., None]).astype(jnp.bfloat16)
    local_state = jnp.einsum(
        "sghp,sgn->ghpn", weighted, in_maps, preferred_element_type=jnp.float32
    )
    block_log_decay = cumul[..., -1]

    incoming = carried_scan(local_state, block_log_decay, position, ctx_count)

    attention_out = causal_attention(position, queries, same_core_kv, other_core_kv)

    carried_out = jnp.einsum(
        "ghpn,tgn->tghp", incoming, out_maps.astype(jnp.float32), precision=lax.Precision.HIGHEST
    )
    carried_out = carried_out * jnp.exp(cumul).transpose(2, 0, 1)[..., None]
    direct = skip_gain.reshape(groups_local, heads_group)[None, :, :, None] * mixer_in.astype(
        jnp.float32
    )
    outputs = (inner + carried_out + direct).reshape(tok_rows, -1)
    gated = outputs * jax.nn.silu(gate_input.astype(jnp.float32))
    square_total = summed_over(jnp.sum(gated * gated, axis=-1), "tp")
    scaling = lax.rsqrt(square_total / (STATE_HEADS * P_SIZE) + 1e-05)
    mixer_out = (gated * scaling[:, None] * norm_gain.astype(jnp.float32)).astype(jnp.bfloat16)
    return (attention_out, mixer_out)


def solution(mesh):
    placed = (
        P("ctx", "tp"),
        P("ctx", "tp"),
        P("ctx", "tp"),
        P("ctx", "tp"),
        P("ctx", "tp"),
        P("ctx", "tp"),
        P("ctx", "tp"),
        P("tp", "ctx"),
        P("tp", "ctx"),
        P("tp"),
        P("tp"),
    )
    ctx_count = mesh.shape["ctx"]
    fine_mesh = jax.sharding.Mesh(
        mesh.devices.reshape(ctx_count // 2, 2, mesh.shape["tp"]), ("chip", "core", "tp")
    )
    ctx = ("chip", "core")
    placed = tuple(P(*[ctx if axis == "ctx" else axis for axis in spec]) for spec in placed)

    def fine_local(*args):
        return local(*args)

    return jax.shard_map(
        fine_local,
        mesh=fine_mesh,
        in_specs=placed,
        out_specs=(P(ctx, "tp"), P(ctx, "tp")),
        check_vma=False,
    )
```

```python
import functools

import jax
import jax.numpy as jnp
from jax import lax
from jax.experimental import pallas as pl
from jax.experimental.pallas import tpu as pltpu
from jax.sharding import PartitionSpec as P

HEAD_WIDTH = 128
STATE_HEADS = 128
P_SIZE = 64
N = 128


causal_score = -1e30


def attend_kernel(pos_ref, qt_ref, kv_ref, o_ref, p_sc, m_sc, l_sc, c_sc, acc_sc, *, tok, width, chunk):
    position = pos_ref[0]
    score_factor = width ** (-0.5)
    rows = qt_ref.shape[1]
    block_rows = kv_ref.shape[2]
    m_sc[...] = jnp.full(m_sc.shape, causal_score, jnp.float32)
    l_sc[...] = jnp.zeros(l_sc.shape, jnp.float32)
    acc_sc[...] = jnp.zeros(acc_sc.shape, jnp.float32)

    def run_block(kb, masked):
        key_portion = kv_ref[kb, 0]
        for c in range(rows // chunk):
            r0 = c * chunk
            score_t = jnp.dot(key_portion, qt_ref[:, r0:r0 + chunk],
                              preferred_element_type=jnp.float32) * score_factor
            if masked:
                key_idx = lax.broadcasted_iota(jnp.int32, (block_rows, chunk), 0)
                query_idx = (r0 % tok) + lax.broadcasted_iota(jnp.int32, (block_rows, chunk), 1)
                is_valid = key_idx <= query_idx
                score_t = jnp.where(is_valid, score_t, causal_score)
            run_max = m_sc[:, r0:r0 + chunk]
            new_max = jnp.maximum(run_max, jnp.max(score_t, axis=0, keepdims=True))
            weights = jnp.exp(score_t - new_max)
            if masked:
                weights = jnp.where(is_valid, weights, 0.0)
            correction_factor = jnp.exp(run_max - new_max)
            l_sc[:, r0:r0 + chunk] = l_sc[:, r0:r0 + chunk] * correction_factor + jnp.sum(weights, axis=0, keepdims=True)
            m_sc[:, r0:r0 + chunk] = new_max
            c_sc[:, r0:r0 + chunk] = correction_factor
            p_sc[:, r0:r0 + chunk] = weights.astype(jnp.bfloat16)
        acc_sc[...] = acc_sc[...] * c_sc[...] + lax.dot_general(kv_ref[kb, 1], p_sc[...], (((0,), (0,)), ((), ())), preferred_element_type=jnp.float32)

    def body(kb, carry):
        run_block(kb, False)
        return carry
    lax.fori_loop(0, position, body, 0)
    run_block(position, True)
    o_ref[...] = (acc_sc[...] / l_sc[...]).astype(o_ref.dtype)


def causal_attention(position, queries, gathered_kv, chunk=256):
    blocks, _, tok_rows, width = gathered_kv.shape
    heads = queries.shape[1] // width
    rows = heads * tok_rows
    queries_t = queries.reshape(tok_rows, heads, width).transpose(2, 1, 0).reshape(width, rows)
    kernel = functools.partial(attend_kernel, tok=tok_rows, width=width, chunk=chunk)
    out_t = pl.pallas_call(
        kernel,
        in_specs=[pl.BlockSpec(memory_space=pltpu.SMEM)] + [pl.BlockSpec(memory_space=pltpu.VMEM)] * 2,
        out_specs=pl.BlockSpec(memory_space=pltpu.VMEM),
        out_shape=jax.ShapeDtypeStruct((width, rows), queries.dtype),
        scratch_shapes=[
            pltpu.VMEM((tok_rows, rows), jnp.bfloat16),
            pltpu.VMEM((1, rows), jnp.float32),
            pltpu.VMEM((1, rows), jnp.float32),
            pltpu.VMEM((1, rows), jnp.float32),
            pltpu.VMEM((width, rows), jnp.float32),
        ],
    )(position.reshape(1), queries_t, gathered_kv)
    return out_t.reshape(width, heads, tok_rows).transpose(2, 1, 0).reshape(tok_rows, heads * width)


def shifted(block, axis, distance):
    devices = range(lax.axis_size(axis))
    route = [(i - distance, i) for i in devices if i - distance in devices]
    return lax.ppermute(block, axis, route)


def summed_over(part, axis):
    count = lax.axis_size(axis)
    total = part
    distance = 1
    while distance < count:
        route = [(i, i ^ distance) for i in range(count)]
        total = total + lax.ppermute(total, axis, route)
        distance *= 2
    return total


def packed(state, log_span):
    heads = log_span.shape[-1]
    lanes = state.shape[-1]
    rows = state.astype(jnp.bfloat16).reshape(state.shape[0], -1, lanes)
    high = lax.reduce_precision(log_span, exponent_bits=8, mantissa_bits=7)
    rest = log_span - high
    middle = lax.reduce_precision(rest, exponent_bits=8, mantissa_bits=7)
    low = rest - middle
    parts = jnp.stack((high, middle, low), axis=1).astype(jnp.bfloat16)
    tail = jnp.pad(parts, ((0, 0), (0, 16 - parts.shape[1]), (0, lanes - heads)))
    return jnp.concatenate((rows, tail), axis=1)


def unpacked(block, state_shape):
    heads = state_shape[1]
    body_rows = block.shape[1] - 16
    state = block[:, :body_rows].reshape(state_shape).astype(jnp.float32)
    parts = block[:, body_rows:body_rows + 3, :heads].astype(jnp.float32)
    return state, (parts[:, 0] + parts[:, 1]) + parts[:, 2]


def carried_scan(local_state, block_log_decay, position, ctx_count):
    sent = packed(local_state, block_log_decay)
    one_back_state, one_back_decay = unpacked(shifted(sent, "ctx", 1), local_state.shape)
    two_back_state, two_back_decay = unpacked(shifted(sent, "ctx", 2), local_state.shape)
    state = jnp.exp(one_back_decay)[..., None, None] * two_back_state + one_back_state
    log_span = one_back_decay + two_back_decay
    distance = 2
    while distance < ctx_count:
        earlier_state, earlier_span = unpacked(
            shifted(packed(state, log_span), "ctx", distance), local_state.shape
        )
        state = jnp.exp(log_span)[..., None, None] * earlier_state + state
        log_span = log_span + earlier_span
        distance *= 2
    return state


def local(
    queries,
    key_rows,
    value_head_rows,
    ssm_input,
    gate_input,
    b_matrix,
    c_matrix,
    step_size,
    log_decay,
    skip_gain,
    norm_gain,
):
    tok_rows = queries.shape[0]
    ctx_count = lax.axis_size("ctx")
    position = lax.axis_index("ctx")

    gathered_kv = lax.all_gather(jnp.stack((key_rows, value_head_rows)), "ctx")

    heads_local = step_size.shape[0]
    groups_local = b_matrix.shape[1] // N
    heads_group = heads_local // groups_local
    mixer_in = ssm_input.reshape(tok_rows, groups_local, heads_group, P_SIZE)
    in_maps = b_matrix.reshape(tok_rows, groups_local, N)
    out_maps = c_matrix.reshape(tok_rows, groups_local, N)
    steps_here = step_size.reshape(groups_local, heads_group, tok_rows)
    cumul = jnp.cumsum(log_decay.reshape(groups_local, heads_group, tok_rows), axis=-1)
    causal = jnp.tril(jnp.ones((tok_rows, tok_rows), dtype=bool))
    gram = jnp.einsum("tgn,sgn->gts", out_maps, in_maps, preferred_element_type=jnp.float32)
    spread = jnp.where(causal, cumul[..., :, None] - cumul[..., None, :], 0.0)
    mixing = jnp.where(
        causal, gram[:, None] * jnp.exp(spread) * steps_here[..., None, :], 0.0
    ).astype(jnp.bfloat16)
    inner = jnp.einsum("ghts,sghp->tghp", mixing, mixer_in, preferred_element_type=jnp.float32)
    weight_end = jnp.exp(cumul[..., -1:] - cumul) * steps_here
    weighted = (mixer_in * weight_end.transpose(2, 0, 1)[..., None]).astype(jnp.bfloat16)
    local_state = jnp.einsum(
        "sghp,sgn->ghpn", weighted, in_maps, preferred_element_type=jnp.float32
    )
    block_log_decay = cumul[..., -1]

    incoming = carried_scan(local_state, block_log_decay, position, ctx_count)

    incoming, gathered_kv = lax.optimization_barrier((incoming, gathered_kv))
    attention_out = causal_attention(position, queries, gathered_kv)

    carried_out = jnp.einsum(
        "ghpn,tgn->tghp", incoming, out_maps.astype(jnp.float32), precision=lax.Precision.HIGHEST
    )
    carried_out = carried_out * jnp.exp(cumul).transpose(2, 0, 1)[..., None]
    direct = skip_gain.reshape(groups_local, heads_group)[None, :, :, None] * mixer_in.astype(
        jnp.float32
    )
    outputs = (inner + carried_out + direct).reshape(tok_rows, -1)
    gated = outputs * jax.nn.silu(gate_input.astype(jnp.float32))
    square_part, attention_out = lax.optimization_barrier((jnp.sum(gated * gated, axis=-1), attention_out))
    square_total = summed_over(square_part, "tp")
    scaling = lax.rsqrt(square_total / (STATE_HEADS * P_SIZE) + 1e-05)
    mixer_out = (gated * scaling[:, None] * norm_gain.astype(jnp.float32)).astype(jnp.bfloat16)
    return (attention_out, mixer_out)


def solution(mesh):
    placed = (
        P("ctx", "tp"),
        P("ctx", "tp"),
        P("ctx", "tp"),
        P("ctx", "tp"),
        P("ctx", "tp"),
        P("ctx", "tp"),
        P("ctx", "tp"),
        P("tp", "ctx"),
        P("tp", "ctx"),
        P("tp"),
        P("tp"),
    )
    return jax.shard_map(
        local,
        mesh=mesh,
        in_specs=placed,
        out_specs=(P("ctx", "tp"), P("ctx", "tp")),
        check_vma=False,
    )
```

```python
import functools

import jax
import jax.numpy as jnp
from jax import lax
from jax.experimental import pallas as pl
from jax.experimental.pallas import tpu as pltpu
from jax.sharding import PartitionSpec as P

HEAD_WIDTH = 128
STATE_HEADS = 128
P_SIZE = 64
N = 128


causal_score = -1e30


def attend_kernel(pos_ref, qt_ref, kv_ref, o_ref, p_sc, m_sc, l_sc, c_sc, acc_sc, *, tok, width, chunk):
    position = pos_ref[0]
    score_factor = width ** (-0.5)
    rows = qt_ref.shape[1]
    block_rows = kv_ref.shape[2]
    m_sc[...] = jnp.full(m_sc.shape, causal_score, jnp.float32)
    l_sc[...] = jnp.zeros(l_sc.shape, jnp.float32)
    acc_sc[...] = jnp.zeros(acc_sc.shape, jnp.float32)

    def run_block(kb, masked):
        key_portion = kv_ref[kb, 0]
        for c in range(rows // chunk):
            r0 = c * chunk
            score_t = jnp.dot(key_portion, qt_ref[:, r0:r0 + chunk],
                              preferred_element_type=jnp.float32) * score_factor
            if masked:
                key_idx = lax.broadcasted_iota(jnp.int32, (block_rows, chunk), 0)
                query_idx = (r0 % tok) + lax.broadcasted_iota(jnp.int32, (block_rows, chunk), 1)
                is_valid = key_idx <= query_idx
                score_t = jnp.where(is_valid, score_t, causal_score)
            run_max = m_sc[:, r0:r0 + chunk]
            new_max = jnp.maximum(run_max, jnp.max(score_t, axis=0, keepdims=True))
            weights = jnp.exp(score_t - new_max)
            if masked:
                weights = jnp.where(is_valid, weights, 0.0)
            correction_factor = jnp.exp(run_max - new_max)
            l_sc[:, r0:r0 + chunk] = l_sc[:, r0:r0 + chunk] * correction_factor + jnp.sum(weights, axis=0, keepdims=True)
            m_sc[:, r0:r0 + chunk] = new_max
            c_sc[:, r0:r0 + chunk] = correction_factor
            p_sc[:, r0:r0 + chunk] = weights.astype(jnp.bfloat16)
        acc_sc[...] = acc_sc[...] * c_sc[...] + lax.dot_general(kv_ref[kb, 1], p_sc[...], (((0,), (0,)), ((), ())), preferred_element_type=jnp.float32)

    def body(kb, carry):
        run_block(kb, False)
        return carry
    lax.fori_loop(0, position, body, 0)
    run_block(position, True)
    o_ref[...] = (acc_sc[...] / l_sc[...]).astype(o_ref.dtype)


def causal_attention(position, queries, gathered_kv, chunk=256):
    blocks, _, tok_rows, width = gathered_kv.shape
    heads = queries.shape[1] // width
    rows = heads * tok_rows
    queries_t = queries.reshape(tok_rows, heads, width).transpose(2, 1, 0).reshape(width, rows)
    kernel = functools.partial(attend_kernel, tok=tok_rows, width=width, chunk=chunk)
    out_t = pl.pallas_call(
        kernel,
        in_specs=[pl.BlockSpec(memory_space=pltpu.SMEM)] + [pl.BlockSpec(memory_space=pltpu.VMEM)] * 2,
        out_specs=pl.BlockSpec(memory_space=pltpu.VMEM),
        out_shape=jax.ShapeDtypeStruct((width, rows), queries.dtype),
        scratch_shapes=[
            pltpu.VMEM((tok_rows, rows), jnp.bfloat16),
            pltpu.VMEM((1, rows), jnp.float32),
            pltpu.VMEM((1, rows), jnp.float32),
            pltpu.VMEM((1, rows), jnp.float32),
            pltpu.VMEM((width, rows), jnp.float32),
        ],
        cost_estimate=pl.CostEstimate(
            flops=4 * rows * width * tok_rows * blocks,
            transcendentals=rows * tok_rows * blocks,
            bytes_accessed=2 * (queries.size * 2 + gathered_kv.size),
        ),
    )(position.reshape(1), queries_t, gathered_kv)
    return out_t.reshape(width, heads, tok_rows).transpose(2, 1, 0).reshape(tok_rows, heads * width)


def shifted(block, axis, distance):
    devices = range(lax.axis_size(axis))
    route = [(i - distance, i) for i in devices if i - distance in devices]
    return lax.ppermute(block, axis, route)


def summed_over(part, axis):
    count = lax.axis_size(axis)
    total = part
    for distance in range(1, count):
        route = [(i, (i + distance) % count) for i in range(count)]
        total = total + lax.ppermute(part, axis, route)
    return total


def packed(state, log_span):
    heads = log_span.shape[-1]
    lanes = state.shape[-1]
    rows = state.astype(jnp.bfloat16).reshape(state.shape[0], -1, lanes)
    high = lax.reduce_precision(log_span, exponent_bits=8, mantissa_bits=7)
    rest = log_span - high
    middle = lax.reduce_precision(rest, exponent_bits=8, mantissa_bits=7)
    low = rest - middle
    parts = jnp.stack((high, middle, low), axis=1).astype(jnp.bfloat16)
    tail = jnp.pad(parts, ((0, 0), (0, 16 - parts.shape[1]), (0, lanes - heads)))
    return jnp.concatenate((rows, tail), axis=1)


def unpacked(block, state_shape):
    heads = state_shape[1]
    body_rows = block.shape[1] - 16
    state = block[:, :body_rows].reshape(state_shape).astype(jnp.float32)
    parts = block[:, body_rows:body_rows + 3, :heads].astype(jnp.float32)
    return state, (parts[:, 0] + parts[:, 1]) + parts[:, 2]


def carried_scan(local_state, block_log_decay, position, ctx_count):
    sent = packed(local_state, block_log_decay)
    one_back_state, one_back_decay = unpacked(shifted(sent, "ctx", 1), local_state.shape)
    two_back_state, two_back_decay = unpacked(shifted(sent, "ctx", 2), local_state.shape)
    state = jnp.exp(one_back_decay)[..., None, None] * two_back_state + one_back_state
    log_span = one_back_decay + two_back_decay
    distance = 2
    while distance < ctx_count:
        earlier_state, earlier_span = unpacked(
            shifted(packed(state, log_span), "ctx", distance), local_state.shape
        )
        state = jnp.exp(log_span)[..., None, None] * earlier_state + state
        log_span = log_span + earlier_span
        distance *= 2
    return state


def local(
    queries,
    key_rows,
    value_head_rows,
    ssm_input,
    gate_input,
    b_matrix,
    c_matrix,
    step_size,
    log_decay,
    skip_gain,
    norm_gain,
):
    tok_rows = queries.shape[0]
    ctx_count = lax.axis_size("ctx")
    position = lax.axis_index("ctx")

    gathered_kv = lax.all_gather(jnp.stack((key_rows, value_head_rows)), "ctx")

    heads_local = step_size.shape[0]
    groups_local = b_matrix.shape[1] // N
    heads_group = heads_local // groups_local
    mixer_in = ssm_input.reshape(tok_rows, groups_local, heads_group, P_SIZE)
    in_maps = b_matrix.reshape(tok_rows, groups_local, N)
    out_maps = c_matrix.reshape(tok_rows, groups_local, N)
    steps_here = step_size.reshape(groups_local, heads_group, tok_rows)
    cumul = jnp.cumsum(log_decay.reshape(groups_local, heads_group, tok_rows), axis=-1)
    causal = jnp.tril(jnp.ones((tok_rows, tok_rows), dtype=bool))
    gram = jnp.einsum("tgn,sgn->gts", out_maps, in_maps, preferred_element_type=jnp.float32)
    spread = jnp.where(causal, cumul[..., :, None] - cumul[..., None, :], 0.0)
    mixing = jnp.where(
        causal, gram[:, None] * jnp.exp(spread) * steps_here[..., None, :], 0.0
    ).astype(jnp.bfloat16)
    inner = jnp.einsum("ghts,sghp->tghp", mixing, mixer_in, preferred_element_type=jnp.float32)
    weight_end = jnp.exp(cumul[..., -1:] - cumul) * steps_here
    weighted = (mixer_in * weight_end.transpose(2, 0, 1)[..., None]).astype(jnp.bfloat16)
    local_state = jnp.einsum(
        "sghp,sgn->ghpn", weighted, in_maps, preferred_element_type=jnp.float32
    )
    block_log_decay = cumul[..., -1]

    incoming = carried_scan(local_state, block_log_decay, position, ctx_count)

    incoming, gathered_kv = lax.optimization_barrier((incoming, gathered_kv))
    attention_out = causal_attention(position, queries, gathered_kv)

    carried_out = jnp.einsum(
        "ghpn,tgn->tghp", incoming, out_maps.astype(jnp.float32), precision=lax.Precision.HIGHEST
    )
    carried_out = carried_out * jnp.exp(cumul).transpose(2, 0, 1)[..., None]
    direct = skip_gain.reshape(groups_local, heads_group)[None, :, :, None] * mixer_in.astype(
        jnp.float32
    )
    outputs = (inner + carried_out + direct).reshape(tok_rows, -1)
    gated = outputs * jax.nn.silu(gate_input.astype(jnp.float32))
    square_total = summed_over(jnp.sum(gated * gated, axis=-1), "tp")
    scaling = lax.rsqrt(square_total / (STATE_HEADS * P_SIZE) + 1e-05)
    mixer_out = (gated * scaling[:, None] * norm_gain.astype(jnp.float32)).astype(jnp.bfloat16)
    return (attention_out, mixer_out)


def solution(mesh):
    placed = (
        P("ctx", "tp"),
        P("ctx", "tp"),
        P("ctx", "tp"),
        P("ctx", "tp"),
        P("ctx", "tp"),
        P("ctx", "tp"),
        P("ctx", "tp"),
        P("tp", "ctx"),
        P("tp", "ctx"),
        P("tp"),
        P("tp"),
    )
    return jax.shard_map(
        local,
        mesh=mesh,
        in_specs=placed,
        out_specs=(P("ctx", "tp"), P("ctx", "tp")),
        check_vma=False,
    )
```

```python
import functools

import jax
import jax.numpy as jnp
from jax import lax
from jax.experimental import pallas as pl
from jax.experimental.pallas import tpu as pltpu
from jax.sharding import PartitionSpec as P

HEAD_WIDTH = 128
STATE_HEADS = 128
P_SIZE = 64
N = 128


causal_score = -1e30


def attend_kernel(pos_ref, qt_ref, kv_ref, o_ref, p_sc, m_sc, l_sc, c_sc, acc_sc, *, tok, width, chunk):
    position = pos_ref[0]
    score_factor = width ** (-0.5)
    rows = qt_ref.shape[1]
    block_rows = kv_ref.shape[2]
    m_sc[...] = jnp.full(m_sc.shape, causal_score, jnp.float32)
    l_sc[...] = jnp.zeros(l_sc.shape, jnp.float32)
    acc_sc[...] = jnp.zeros(acc_sc.shape, jnp.float32)

    def run_block(kb, masked):
        key_portion = kv_ref[kb, 0]
        for c in range(rows // chunk):
            r0 = c * chunk
            score_t = jnp.dot(key_portion, qt_ref[:, r0:r0 + chunk],
                              preferred_element_type=jnp.float32) * score_factor
            if masked:
                key_idx = lax.broadcasted_iota(jnp.int32, (block_rows, chunk), 0)
                query_idx = (r0 % tok) + lax.broadcasted_iota(jnp.int32, (block_rows, chunk), 1)
                is_valid = key_idx <= query_idx
                score_t = jnp.where(is_valid, score_t, causal_score)
            run_max = m_sc[:, r0:r0 + chunk]
            new_max = jnp.maximum(run_max, jnp.max(score_t, axis=0, keepdims=True))
            weights = jnp.exp(score_t - new_max)
            if masked:
                weights = jnp.where(is_valid, weights, 0.0)
            correction_factor = jnp.exp(run_max - new_max)
            l_sc[:, r0:r0 + chunk] = l_sc[:, r0:r0 + chunk] * correction_factor + jnp.sum(weights, axis=0, keepdims=True)
            m_sc[:, r0:r0 + chunk] = new_max
            c_sc[:, r0:r0 + chunk] = correction_factor
            p_sc[:, r0:r0 + chunk] = weights.astype(jnp.bfloat16)
        acc_sc[...] = acc_sc[...] * c_sc[...] + lax.dot_general(kv_ref[kb, 1], p_sc[...], (((0,), (0,)), ((), ())), preferred_element_type=jnp.float32)

    def body(kb, carry):
        run_block(kb, False)
        return carry
    lax.fori_loop(0, position, body, 0)
    run_block(position, True)
    o_ref[...] = (acc_sc[...] / l_sc[...]).astype(o_ref.dtype)


def causal_attention(position, queries, gathered_kv, chunk=256):
    blocks, _, tok_rows, width = gathered_kv.shape
    heads = queries.shape[1] // width
    rows = heads * tok_rows
    queries_t = queries.reshape(tok_rows, heads, width).transpose(2, 1, 0).reshape(width, rows)
    kernel = functools.partial(attend_kernel, tok=tok_rows, width=width, chunk=chunk)
    out_t = pl.pallas_call(
        kernel,
        in_specs=[pl.BlockSpec(memory_space=pltpu.SMEM)] + [pl.BlockSpec(memory_space=pltpu.VMEM)] * 2,
        out_specs=pl.BlockSpec(memory_space=pltpu.VMEM),
        out_shape=jax.ShapeDtypeStruct((width, rows), queries.dtype),
        scratch_shapes=[
            pltpu.VMEM((tok_rows, rows), jnp.bfloat16),
            pltpu.VMEM((1, rows), jnp.float32),
            pltpu.VMEM((1, rows), jnp.float32),
            pltpu.VMEM((1, rows), jnp.float32),
            pltpu.VMEM((width, rows), jnp.float32),
        ],
        cost_estimate=pl.CostEstimate(
            flops=4 * rows * width * tok_rows * blocks,
            transcendentals=rows * tok_rows * blocks,
            bytes_accessed=2 * (queries.size * 2 + gathered_kv.size),
        ),
    )(position.reshape(1), queries_t, gathered_kv)
    return out_t.reshape(width, heads, tok_rows).transpose(2, 1, 0).reshape(tok_rows, heads * width)


def shifted(block, axis, distance):
    devices = range(lax.axis_size(axis))
    route = [(i - distance, i) for i in devices if i - distance in devices]
    return lax.ppermute(block, axis, route)


def padded(part, width=16384):
    return jnp.zeros((width,), part.dtype).at[: part.shape[0]].set(part)


def packed(state, log_span):
    heads = log_span.shape[-1]
    lanes = state.shape[-1]
    rows = state.astype(jnp.bfloat16).reshape(state.shape[0], -1, lanes)
    high = lax.reduce_precision(log_span, exponent_bits=8, mantissa_bits=7)
    rest = log_span - high
    middle = lax.reduce_precision(rest, exponent_bits=8, mantissa_bits=7)
    low = rest - middle
    parts = jnp.stack((high, middle, low), axis=1).astype(jnp.bfloat16)
    tail = jnp.pad(parts, ((0, 0), (0, 16 - parts.shape[1]), (0, lanes - heads)))
    return jnp.concatenate((rows, tail), axis=1)


def unpacked(block, state_shape):
    heads = state_shape[1]
    body_rows = block.shape[1] - 16
    state = block[:, :body_rows].reshape(state_shape).astype(jnp.float32)
    parts = block[:, body_rows:body_rows + 3, :heads].astype(jnp.float32)
    return state, (parts[:, 0] + parts[:, 1]) + parts[:, 2]


def carried_scan(local_state, block_log_decay, position, ctx_count):
    sent = packed(local_state, block_log_decay)
    one_back_state, one_back_decay = unpacked(shifted(sent, "ctx", 1), local_state.shape)
    two_back_state, two_back_decay = unpacked(shifted(sent, "ctx", 2), local_state.shape)
    state = jnp.exp(one_back_decay)[..., None, None] * two_back_state + one_back_state
    log_span = one_back_decay + two_back_decay
    distance = 2
    while distance < ctx_count:
        earlier_state, earlier_span = unpacked(
            shifted(packed(state, log_span), "ctx", distance), local_state.shape
        )
        state = jnp.exp(log_span)[..., None, None] * earlier_state + state
        log_span = log_span + earlier_span
        distance *= 2
    return state


def local(
    queries,
    key_rows,
    value_head_rows,
    ssm_input,
    gate_input,
    b_matrix,
    c_matrix,
    step_size,
    log_decay,
    skip_gain,
    norm_gain,
):
    tok_rows = queries.shape[0]
    ctx_count = lax.axis_size("ctx")
    position = lax.axis_index("ctx")

    gathered_kv = lax.all_gather(jnp.stack((key_rows, value_head_rows)), "ctx")

    heads_local = step_size.shape[0]
    groups_local = b_matrix.shape[1] // N
    heads_group = heads_local // groups_local
    mixer_in = ssm_input.reshape(tok_rows, groups_local, heads_group, P_SIZE)
    in_maps = b_matrix.reshape(tok_rows, groups_local, N)
    out_maps = c_matrix.reshape(tok_rows, groups_local, N)
    steps_here = step_size.reshape(groups_local, heads_group, tok_rows)
    cumul = jnp.cumsum(log_decay.reshape(groups_local, heads_group, tok_rows), axis=-1)
    causal = jnp.tril(jnp.ones((tok_rows, tok_rows), dtype=bool))
    gram = jnp.einsum("tgn,sgn->gts", out_maps, in_maps, preferred_element_type=jnp.float32)
    spread = jnp.where(causal, cumul[..., :, None] - cumul[..., None, :], 0.0)
    mixing = jnp.where(
        causal, gram[:, None] * jnp.exp(spread) * steps_here[..., None, :], 0.0
    ).astype(jnp.bfloat16)
    inner = jnp.einsum("ghts,sghp->tghp", mixing, mixer_in, preferred_element_type=jnp.float32)
    weight_end = jnp.exp(cumul[..., -1:] - cumul) * steps_here
    weighted = (mixer_in * weight_end.transpose(2, 0, 1)[..., None]).astype(jnp.bfloat16)
    local_state = jnp.einsum(
        "sghp,sgn->ghpn", weighted, in_maps, preferred_element_type=jnp.float32
    )
    block_log_decay = cumul[..., -1]

    incoming = carried_scan(local_state, block_log_decay, position, ctx_count)


    carried_out = jnp.einsum(
        "ghpn,tgn->tghp", incoming, out_maps.astype(jnp.float32), precision=lax.Precision.HIGHEST
    )
    carried_out = carried_out * jnp.exp(cumul).transpose(2, 0, 1)[..., None]
    direct = skip_gain.reshape(groups_local, heads_group)[None, :, :, None] * mixer_in.astype(
        jnp.float32
    )
    outputs = (inner + carried_out + direct).reshape(tok_rows, -1)
    gated = outputs * jax.nn.silu(gate_input.astype(jnp.float32))
    square_parts, gathered_kv = lax.optimization_barrier(
        (padded(jnp.sum(gated * gated, axis=-1)), gathered_kv)
    )
    square_total = lax.psum(square_parts, "tp")[:tok_rows]
    attention_out = causal_attention(position, queries, gathered_kv)
    scaling = lax.rsqrt(square_total / (STATE_HEADS * P_SIZE) + 1e-05)
    mixer_out = (gated * scaling[:, None] * norm_gain.astype(jnp.float32)).astype(jnp.bfloat16)
    return (attention_out, mixer_out)


def solution(mesh):
    placed = (
        P("ctx", "tp"),
        P("ctx", "tp"),
        P("ctx", "tp"),
        P("ctx", "tp"),
        P("ctx", "tp"),
        P("ctx", "tp"),
        P("ctx", "tp"),
        P("tp", "ctx"),
        P("tp", "ctx"),
        P("tp"),
        P("tp"),
    )
    return jax.shard_map(
        local,
        mesh=mesh,
        in_specs=placed,
        out_specs=(P("ctx", "tp"), P("ctx", "tp")),
        check_vma=False,
    )
```

```python
import functools

import jax
import jax.numpy as jnp
from jax import lax
from jax.experimental import pallas as pl
from jax.experimental.pallas import tpu as pltpu
from jax.sharding import PartitionSpec as P

HEAD_WIDTH = 128
STATE_HEADS = 128
P_SIZE = 64
N = 128


causal_score = -1e30
CTX = ("chip", "core")


def attend_kernel(pos_ref, qt_ref, kv_ref, o_ref, p_sc, m_sc, l_sc, c_sc, acc_sc, *, tok, width, chunk):
    position = pos_ref[0]
    score_factor = width ** (-0.5)
    rows = qt_ref.shape[1]
    block_rows = kv_ref.shape[2]
    m_sc[...] = jnp.full(m_sc.shape, causal_score, jnp.float32)
    l_sc[...] = jnp.zeros(l_sc.shape, jnp.float32)
    acc_sc[...] = jnp.zeros(acc_sc.shape, jnp.float32)

    def run_block(kb, masked):
        key_portion = kv_ref[kb, 0]
        for c in range(rows // chunk):
            r0 = c * chunk
            score_t = jnp.dot(key_portion, qt_ref[:, r0:r0 + chunk],
                              preferred_element_type=jnp.float32) * score_factor
            if masked:
                key_idx = lax.broadcasted_iota(jnp.int32, (block_rows, chunk), 0)
                query_idx = (r0 % tok) + lax.broadcasted_iota(jnp.int32, (block_rows, chunk), 1)
                is_valid = key_idx <= query_idx
                score_t = jnp.where(is_valid, score_t, causal_score)
            run_max = m_sc[:, r0:r0 + chunk]
            new_max = jnp.maximum(run_max, jnp.max(score_t, axis=0, keepdims=True))
            weights = jnp.exp(score_t - new_max)
            if masked:
                weights = jnp.where(is_valid, weights, 0.0)
            correction_factor = jnp.exp(run_max - new_max)
            l_sc[:, r0:r0 + chunk] = l_sc[:, r0:r0 + chunk] * correction_factor + jnp.sum(weights, axis=0, keepdims=True)
            m_sc[:, r0:r0 + chunk] = new_max
            c_sc[:, r0:r0 + chunk] = correction_factor
            p_sc[:, r0:r0 + chunk] = weights.astype(jnp.bfloat16)
        acc_sc[...] = acc_sc[...] * c_sc[...] + lax.dot_general(kv_ref[kb, 1], p_sc[...], (((0,), (0,)), ((), ())), preferred_element_type=jnp.float32)

    def body(kb, carry):
        run_block(kb, False)
        return carry
    lax.fori_loop(0, position, body, 0)
    run_block(position, True)
    o_ref[...] = (acc_sc[...] / l_sc[...]).astype(o_ref.dtype)


def causal_attention(position, queries, gathered_kv, chunk=256):
    blocks, _, tok_rows, width = gathered_kv.shape
    heads = queries.shape[1] // width
    rows = heads * tok_rows
    queries_t = queries.reshape(tok_rows, heads, width).transpose(2, 1, 0).reshape(width, rows)
    kernel = functools.partial(attend_kernel, tok=tok_rows, width=width, chunk=chunk)
    out_t = pl.pallas_call(
        kernel,
        in_specs=[pl.BlockSpec(memory_space=pltpu.SMEM)] + [pl.BlockSpec(memory_space=pltpu.VMEM)] * 2,
        out_specs=pl.BlockSpec(memory_space=pltpu.VMEM),
        out_shape=jax.ShapeDtypeStruct((width, rows), queries.dtype),
        scratch_shapes=[
            pltpu.VMEM((tok_rows, rows), jnp.bfloat16),
            pltpu.VMEM((1, rows), jnp.float32),
            pltpu.VMEM((1, rows), jnp.float32),
            pltpu.VMEM((1, rows), jnp.float32),
            pltpu.VMEM((width, rows), jnp.float32),
        ],
    )(position.reshape(1), queries_t, gathered_kv)
    return out_t.reshape(width, heads, tok_rows).transpose(2, 1, 0).reshape(tok_rows, heads * width)


def shifted(block, axis, distance):
    devices = range(lax.axis_size(axis))
    route = [(i - distance, i) for i in devices if i - distance in devices]
    return lax.ppermute(block, axis, route)


def summed_over(part, axis):
    count = lax.axis_size(axis)
    total = part
    distance = 1
    while distance < count:
        route = [(i, i ^ distance) for i in range(count)]
        total = total + lax.ppermute(total, axis, route)
        distance *= 2
    return total


def packed(state, log_span):
    heads = log_span.shape[-1]
    lanes = state.shape[-1]
    rows = state.astype(jnp.bfloat16).reshape(state.shape[0], -1, lanes)
    high = lax.reduce_precision(log_span, exponent_bits=8, mantissa_bits=7)
    rest = log_span - high
    middle = lax.reduce_precision(rest, exponent_bits=8, mantissa_bits=7)
    low = rest - middle
    parts = jnp.stack((high, middle, low), axis=1).astype(jnp.bfloat16)
    tail = jnp.pad(parts, ((0, 0), (0, 16 - parts.shape[1]), (0, lanes - heads)))
    return jnp.concatenate((rows, tail), axis=1)


def unpacked(block, state_shape):
    heads = state_shape[1]
    body_rows = block.shape[1] - 16
    state = block[:, :body_rows].reshape(state_shape).astype(jnp.float32)
    parts = block[:, body_rows:body_rows + 3, :heads].astype(jnp.float32)
    return state, (parts[:, 0] + parts[:, 1]) + parts[:, 2]


def carried_scan(local_state, block_log_decay, axis, count):
    sent = packed(local_state, block_log_decay)
    one_back_state, one_back_decay = unpacked(shifted(sent, axis, 1), local_state.shape)
    two_back_state, two_back_decay = unpacked(shifted(sent, axis, 2), local_state.shape)
    state = jnp.exp(one_back_decay)[..., None, None] * two_back_state + one_back_state
    log_span = one_back_decay + two_back_decay
    distance = 2
    while distance < count:
        earlier_state, earlier_span = unpacked(
            shifted(packed(state, log_span), axis, distance), local_state.shape
        )
        state = jnp.exp(log_span)[..., None, None] * earlier_state + state
        log_span = log_span + earlier_span
        distance *= 2
    return state


def chip_carried_scan(local_state, block_log_decay):
    core = lax.axis_index("core")
    swap = [(0, 1), (1, 0)]
    sent = packed(local_state, block_log_decay)
    own_state, own_decay = unpacked(sent, local_state.shape)
    mate_state, mate_decay = unpacked(lax.ppermute(sent, "core", swap), local_state.shape)
    first_state = jnp.where(core == 0, own_state, mate_state)
    first_decay = jnp.where(core == 0, own_decay, mate_decay)
    second_state = jnp.where(core == 0, mate_state, own_state)
    second_decay = jnp.where(core == 0, mate_decay, own_decay)
    chip_state = jnp.exp(second_decay)[..., None, None] * first_state + second_state
    chip_decay = first_decay + second_decay
    half = local_state.shape[1] // 2
    chip_prefix = carried_scan(
        lax.dynamic_slice_in_dim(chip_state, core * half, half, axis=1),
        lax.dynamic_slice_in_dim(chip_decay, core * half, half, axis=1),
        "chip",
        lax.axis_size("chip"),
    )
    other_prefix = lax.ppermute(chip_prefix.astype(jnp.bfloat16), "core", swap).astype(jnp.float32)
    prefix = jnp.where(
        core == 0,
        jnp.concatenate((chip_prefix, other_prefix), axis=1),
        jnp.concatenate((other_prefix, chip_prefix), axis=1),
    )
    return jnp.where(
        core == 0, prefix, jnp.exp(first_decay)[..., None, None] * prefix + first_state
    )


def local(
    queries,
    key_rows,
    value_head_rows,
    ssm_input,
    gate_input,
    b_matrix,
    c_matrix,
    step_size,
    log_decay,
    skip_gain,
    norm_gain,
):
    tok_rows = queries.shape[0]
    position = lax.axis_index(CTX)

    gathered_kv = lax.all_gather(jnp.stack((key_rows, value_head_rows)), CTX)

    heads_local = step_size.shape[0]
    groups_local = b_matrix.shape[1] // N
    heads_group = heads_local // groups_local
    mixer_in = ssm_input.reshape(tok_rows, groups_local, heads_group, P_SIZE)
    in_maps = b_matrix.reshape(tok_rows, groups_local, N)
    out_maps = c_matrix.reshape(tok_rows, groups_local, N)
    steps_here = step_size.reshape(groups_local, heads_group, tok_rows)
    cumul = jnp.cumsum(log_decay.reshape(groups_local, heads_group, tok_rows), axis=-1)
    causal = jnp.tril(jnp.ones((tok_rows, tok_rows), dtype=bool))
    gram = jnp.einsum("tgn,sgn->gts", out_maps, in_maps, preferred_element_type=jnp.float32)
    spread = jnp.where(causal, cumul[..., :, None] - cumul[..., None, :], 0.0)
    mixing = jnp.where(
        causal, gram[:, None] * jnp.exp(spread) * steps_here[..., None, :], 0.0
    ).astype(jnp.bfloat16)
    inner = jnp.einsum("ghts,sghp->tghp", mixing, mixer_in, preferred_element_type=jnp.float32)
    weight_end = jnp.exp(cumul[..., -1:] - cumul) * steps_here
    weighted = (mixer_in * weight_end.transpose(2, 0, 1)[..., None]).astype(jnp.bfloat16)
    local_state = jnp.einsum(
        "sghp,sgn->ghpn", weighted, in_maps, preferred_element_type=jnp.float32
    )
    block_log_decay = cumul[..., -1]

    incoming = chip_carried_scan(local_state, block_log_decay)

    attention_out = causal_attention(position, queries, gathered_kv)

    carried_out = jnp.einsum(
        "ghpn,tgn->tghp", incoming, out_maps.astype(jnp.float32), precision=lax.Precision.HIGHEST
    )
    carried_out = carried_out * jnp.exp(cumul).transpose(2, 0, 1)[..., None]
    direct = skip_gain.reshape(groups_local, heads_group)[None, :, :, None] * mixer_in.astype(
        jnp.float32
    )
    outputs = (inner + carried_out + direct).reshape(tok_rows, -1)
    gated = outputs * jax.nn.silu(gate_input.astype(jnp.float32))
    square_total = summed_over(jnp.sum(gated * gated, axis=-1), "tp")
    scaling = lax.rsqrt(square_total / (STATE_HEADS * P_SIZE) + 1e-05)
    mixer_out = (gated * scaling[:, None] * norm_gain.astype(jnp.float32)).astype(jnp.bfloat16)
    return (attention_out, mixer_out)


def solution(mesh):
    placed = (
        P("ctx", "tp"),
        P("ctx", "tp"),
        P("ctx", "tp"),
        P("ctx", "tp"),
        P("ctx", "tp"),
        P("ctx", "tp"),
        P("ctx", "tp"),
        P("tp", "ctx"),
        P("tp", "ctx"),
        P("tp"),
        P("tp"),
    )
    fine_mesh = jax.sharding.Mesh(
        mesh.devices.reshape(mesh.shape["ctx"] // 2, 2, mesh.shape["tp"]), CTX + ("tp",)
    )
    placed = tuple(P(*[CTX if axis == "ctx" else axis for axis in spec]) for spec in placed)
    return jax.shard_map(
        local,
        mesh=fine_mesh,
        in_specs=placed,
        out_specs=(P(CTX, "tp"), P(CTX, "tp")),
        check_vma=False,
    )
```

```python
import functools

import jax
import jax.numpy as jnp
from jax import lax
from jax.experimental import pallas as pl
from jax.experimental.pallas import tpu as pltpu
from jax.sharding import PartitionSpec as P

HEAD_WIDTH = 128
STATE_HEADS = 128
P_SIZE = 64
N = 128


causal_score = -1e30
CTX = ("chip", "core")


def attend_kernel(*refs, tok, width, chunk, key_offset, first, last):
    pos_ref, qt_ref, kv_ref = refs[:3]
    rest = list(refs[3:])
    state_in = () if first else (rest.pop(0), rest.pop(0), rest.pop(0))
    outs = (rest.pop(0),) if last else (rest.pop(0), rest.pop(0), rest.pop(0))
    p_sc, m_sc, l_sc, c_sc, acc_sc = rest
    position = pos_ref[0]
    score_factor = width ** (-0.5)
    rows = qt_ref.shape[1]
    block_rows = kv_ref.shape[2]
    if first:
        m_sc[...] = jnp.full(m_sc.shape, causal_score, jnp.float32)
        l_sc[...] = jnp.zeros(l_sc.shape, jnp.float32)
        acc_sc[...] = jnp.zeros(acc_sc.shape, jnp.float32)
    else:
        m_sc[...] = state_in[0][...]
        l_sc[...] = state_in[1][...]
        acc_sc[...] = state_in[2][...]

    def run_block(kb, masked):
        key_portion = kv_ref[kb, 0]
        for c in range(rows // chunk):
            r0 = c * chunk
            score_t = jnp.dot(key_portion, qt_ref[:, r0:r0 + chunk],
                              preferred_element_type=jnp.float32) * score_factor
            if masked:
                key_idx = key_offset + lax.broadcasted_iota(jnp.int32, (block_rows, chunk), 0)
                query_idx = (r0 % tok) + lax.broadcasted_iota(jnp.int32, (block_rows, chunk), 1)
                is_valid = key_idx <= query_idx
                score_t = jnp.where(is_valid, score_t, causal_score)
            run_max = m_sc[:, r0:r0 + chunk]
            new_max = jnp.maximum(run_max, jnp.max(score_t, axis=0, keepdims=True))
            weights = jnp.exp(score_t - new_max)
            if masked:
                weights = jnp.where(is_valid, weights, 0.0)
            correction_factor = jnp.exp(run_max - new_max)
            l_sc[:, r0:r0 + chunk] = l_sc[:, r0:r0 + chunk] * correction_factor + jnp.sum(weights, axis=0, keepdims=True)
            m_sc[:, r0:r0 + chunk] = new_max
            c_sc[:, r0:r0 + chunk] = correction_factor
            p_sc[:, r0:r0 + chunk] = weights.astype(jnp.bfloat16)
        acc_sc[...] = acc_sc[...] * c_sc[...] + lax.dot_general(kv_ref[kb, 1], p_sc[...], (((0,), (0,)), ((), ())), preferred_element_type=jnp.float32)

    def body(kb, carry):
        run_block(kb, False)
        return carry
    lax.fori_loop(0, position, body, 0)
    run_block(position, True)
    if last:
        outs[0][...] = (acc_sc[...] / l_sc[...]).astype(outs[0].dtype)
    else:
        outs[0][...] = m_sc[...]
        outs[1][...] = l_sc[...]
        outs[2][...] = acc_sc[...]


def attend_part(position, queries_t, part_kv, state, key_offset, out_dtype, chunk=256):
    blocks, _, part_rows, width = part_kv.shape
    rows = queries_t.shape[1]
    first, last = state is None, key_offset > 0
    kernel = functools.partial(
        attend_kernel, tok=2 * part_rows, width=width, chunk=chunk,
        key_offset=key_offset, first=first, last=last,
    )
    stats = jax.ShapeDtypeStruct((1, rows), jnp.float32)
    if last:
        out_shape = jax.ShapeDtypeStruct((width, rows), out_dtype)
        out_specs = pl.BlockSpec(memory_space=pltpu.VMEM)
    else:
        out_shape = (stats, stats, jax.ShapeDtypeStruct((width, rows), jnp.float32))
        out_specs = (pl.BlockSpec(memory_space=pltpu.VMEM),) * 3
    operands = (position.reshape(1), queries_t, part_kv) + (() if first else tuple(state))
    return pl.pallas_call(
        kernel,
        in_specs=[pl.BlockSpec(memory_space=pltpu.SMEM)]
        + [pl.BlockSpec(memory_space=pltpu.VMEM)] * (len(operands) - 1),
        out_specs=out_specs,
        out_shape=out_shape,
        scratch_shapes=[
            pltpu.VMEM((part_rows, rows), jnp.bfloat16),
            pltpu.VMEM((1, rows), jnp.float32),
            pltpu.VMEM((1, rows), jnp.float32),
            pltpu.VMEM((1, rows), jnp.float32),
            pltpu.VMEM((width, rows), jnp.float32),
        ],
        cost_estimate=pl.CostEstimate(
            flops=4 * rows * width * part_rows * blocks,
            transcendentals=rows * part_rows * blocks,
            bytes_accessed=2 * (queries_t.size + part_kv.size) + 4 * 4 * rows * width,
        ),
    )(*operands)


def causal_attention(position, queries, first_kv, second_kv):
    tok_rows = queries.shape[0]
    width = first_kv.shape[-1]
    heads = queries.shape[1] // width
    queries_t = queries.reshape(tok_rows, heads, width).transpose(2, 1, 0).reshape(width, -1)
    state = attend_part(position, queries_t, first_kv, None, 0, queries.dtype)
    out_t = attend_part(position, queries_t, second_kv, state, first_kv.shape[2], queries.dtype)
    return out_t.reshape(width, heads, tok_rows).transpose(2, 1, 0).reshape(tok_rows, heads * width)


def shifted(block, axis, distance):
    devices = range(lax.axis_size(axis))
    route = [(i - distance, i) for i in devices if i - distance in devices]
    return lax.ppermute(block, axis, route)


def summed_over(part, axis):
    count = lax.axis_size(axis)
    total = part
    distance = 1
    while distance < count:
        route = [(i, i ^ distance) for i in range(count)]
        total = total + lax.ppermute(total, axis, route)
        distance *= 2
    return total


def packed(state, log_span):
    heads = log_span.shape[-1]
    lanes = state.shape[-1]
    rows = state.astype(jnp.bfloat16).reshape(state.shape[0], -1, lanes)
    high = lax.reduce_precision(log_span, exponent_bits=8, mantissa_bits=7)
    rest = log_span - high
    middle = lax.reduce_precision(rest, exponent_bits=8, mantissa_bits=7)
    low = rest - middle
    parts = jnp.stack((high, middle, low), axis=1).astype(jnp.bfloat16)
    tail = jnp.pad(parts, ((0, 0), (0, 16 - parts.shape[1]), (0, lanes - heads)))
    return jnp.concatenate((rows, tail), axis=1)


def unpacked(block, state_shape):
    heads = state_shape[1]
    body_rows = block.shape[1] - 16
    state = block[:, :body_rows].reshape(state_shape).astype(jnp.float32)
    parts = block[:, body_rows:body_rows + 3, :heads].astype(jnp.float32)
    return state, (parts[:, 0] + parts[:, 1]) + parts[:, 2]


def carried_scan(local_state, block_log_decay, axis, count):
    sent = packed(local_state, block_log_decay)
    one_back_state, one_back_decay = unpacked(shifted(sent, axis, 1), local_state.shape)
    two_back_state, two_back_decay = unpacked(shifted(sent, axis, 2), local_state.shape)
    state = jnp.exp(one_back_decay)[..., None, None] * two_back_state + one_back_state
    log_span = one_back_decay + two_back_decay
    distance = 2
    while distance < count:
        earlier_state, earlier_span = unpacked(
            shifted(packed(state, log_span), axis, distance), local_state.shape
        )
        state = jnp.exp(log_span)[..., None, None] * earlier_state + state
        log_span = log_span + earlier_span
        distance *= 2
    return state


def chip_carried_scan(local_state, block_log_decay):
    core = lax.axis_index("core")
    swap = [(0, 1), (1, 0)]
    sent = packed(local_state, block_log_decay)
    own_state, own_decay = unpacked(sent, local_state.shape)
    mate_state, mate_decay = unpacked(lax.ppermute(sent, "core", swap), local_state.shape)
    first_state = jnp.where(core == 0, own_state, mate_state)
    first_decay = jnp.where(core == 0, own_decay, mate_decay)
    second_state = jnp.where(core == 0, mate_state, own_state)
    second_decay = jnp.where(core == 0, mate_decay, own_decay)
    chip_state = jnp.exp(second_decay)[..., None, None] * first_state + second_state
    chip_decay = first_decay + second_decay
    half = local_state.shape[1] // 2
    chip_prefix = carried_scan(
        lax.dynamic_slice_in_dim(chip_state, core * half, half, axis=1),
        lax.dynamic_slice_in_dim(chip_decay, core * half, half, axis=1),
        "chip",
        lax.axis_size("chip"),
    )
    other_prefix = lax.ppermute(chip_prefix.astype(jnp.bfloat16), "core", swap).astype(jnp.float32)
    prefix = jnp.where(
        core == 0,
        jnp.concatenate((chip_prefix, other_prefix), axis=1),
        jnp.concatenate((other_prefix, chip_prefix), axis=1),
    )
    return jnp.where(
        core == 0, prefix, jnp.exp(first_decay)[..., None, None] * prefix + first_state
    )


def local(
    queries,
    key_rows,
    value_head_rows,
    ssm_input,
    gate_input,
    b_matrix,
    c_matrix,
    step_size,
    log_decay,
    skip_gain,
    norm_gain,
):
    tok_rows = queries.shape[0]
    position = lax.axis_index(CTX)

    local_kv = jnp.stack((key_rows, value_head_rows))
    half_rows = tok_rows // 2
    first_kv = lax.all_gather(local_kv[:, :half_rows], CTX)
    second_kv = lax.all_gather(local_kv[:, half_rows:], CTX)

    heads_local = step_size.shape[0]
    groups_local = b_matrix.shape[1] // N
    heads_group = heads_local // groups_local
    mixer_in = ssm_input.reshape(tok_rows, groups_local, heads_group, P_SIZE)
    in_maps = b_matrix.reshape(tok_rows, groups_local, N)
    out_maps = c_matrix.reshape(tok_rows, groups_local, N)
    steps_here = step_size.reshape(groups_local, heads_group, tok_rows)
    cumul = jnp.cumsum(log_decay.reshape(groups_local, heads_group, tok_rows), axis=-1)
    causal = jnp.tril(jnp.ones((tok_rows, tok_rows), dtype=bool))
    gram = jnp.einsum("tgn,sgn->gts", out_maps, in_maps, preferred_element_type=jnp.float32)
    spread = jnp.where(causal, cumul[..., :, None] - cumul[..., None, :], 0.0)
    mixing = jnp.where(
        causal, gram[:, None] * jnp.exp(spread) * steps_here[..., None, :], 0.0
    ).astype(jnp.bfloat16)
    inner = jnp.einsum("ghts,sghp->tghp", mixing, mixer_in, preferred_element_type=jnp.float32)
    weight_end = jnp.exp(cumul[..., -1:] - cumul) * steps_here
    weighted = (mixer_in * weight_end.transpose(2, 0, 1)[..., None]).astype(jnp.bfloat16)
    local_state = jnp.einsum(
        "sghp,sgn->ghpn", weighted, in_maps, preferred_element_type=jnp.float32
    )
    block_log_decay = cumul[..., -1]

    incoming = chip_carried_scan(local_state, block_log_decay)

    attention_out = causal_attention(position, queries, first_kv, second_kv)

    carried_out = jnp.einsum(
        "ghpn,tgn->tghp", incoming, out_maps.astype(jnp.float32), precision=lax.Precision.HIGHEST
    )
    carried_out = carried_out * jnp.exp(cumul).transpose(2, 0, 1)[..., None]
    direct = skip_gain.reshape(groups_local, heads_group)[None, :, :, None] * mixer_in.astype(
        jnp.float32
    )
    outputs = (inner + carried_out + direct).reshape(tok_rows, -1)
    gated = outputs * jax.nn.silu(gate_input.astype(jnp.float32))
    square_total = summed_over(jnp.sum(gated * gated, axis=-1), "tp")
    scaling = lax.rsqrt(square_total / (STATE_HEADS * P_SIZE) + 1e-05)
    mixer_out = (gated * scaling[:, None] * norm_gain.astype(jnp.float32)).astype(jnp.bfloat16)
    return (attention_out, mixer_out)


def solution(mesh):
    placed = (
        P("ctx", "tp"),
        P("ctx", "tp"),
        P("ctx", "tp"),
        P("ctx", "tp"),
        P("ctx", "tp"),
        P("ctx", "tp"),
        P("ctx", "tp"),
        P("tp", "ctx"),
        P("tp", "ctx"),
        P("tp"),
        P("tp"),
    )
    fine_mesh = jax.sharding.Mesh(
        mesh.devices.reshape(mesh.shape["ctx"] // 2, 2, mesh.shape["tp"]), CTX + ("tp",)
    )
    placed = tuple(P(*[CTX if axis == "ctx" else axis for axis in spec]) for spec in placed)
    return jax.shard_map(
        local,
        mesh=fine_mesh,
        in_specs=placed,
        out_specs=(P(CTX, "tp"), P(CTX, "tp")),
        check_vma=False,
    )
```

```python
import functools

import jax
import jax.numpy as jnp
from jax import lax
from jax.experimental import pallas as pl
from jax.experimental.pallas import tpu as pltpu
from jax.sharding import PartitionSpec as P

HEAD_WIDTH = 128
STATE_HEADS = 128
P_SIZE = 64
N = 128


causal_score = -1e30
CTX = ("chip", "core")


def attend_kernel(pos_ref, qt_ref, kv_ref, o_ref, p_sc, m_sc, l_sc, c_sc, acc_sc, *, tok, width, chunk):
    position = pos_ref[0]
    score_factor = width ** (-0.5) * 1.4426950408889634
    rows = qt_ref.shape[1]
    block_rows = kv_ref.shape[2]
    m_sc[...] = jnp.full(m_sc.shape, causal_score, jnp.float32)
    l_sc[...] = jnp.zeros(l_sc.shape, jnp.float32)
    acc_sc[...] = jnp.zeros(acc_sc.shape, jnp.float32)

    def run_block(kb, masked):
        key_portion = kv_ref[kb, 0]
        for c in range(rows // chunk):
            r0 = c * chunk
            score_t = jnp.dot(key_portion, qt_ref[:, r0:r0 + chunk],
                              preferred_element_type=jnp.float32)
            if masked:
                key_idx = lax.broadcasted_iota(jnp.int32, (block_rows, chunk), 0)
                query_idx = (r0 % tok) + lax.broadcasted_iota(jnp.int32, (block_rows, chunk), 1)
                is_valid = key_idx <= query_idx
                score_t = jnp.where(is_valid, score_t, causal_score)
            run_max = m_sc[:, r0:r0 + chunk]
            new_max = jnp.maximum(run_max, jnp.max(score_t, axis=0, keepdims=True))
            weights = jnp.exp2(score_t * score_factor - new_max * score_factor)
            if masked:
                weights = jnp.where(is_valid, weights, 0.0)
            correction_factor = jnp.exp2((run_max - new_max) * score_factor)
            l_sc[:, r0:r0 + chunk] = l_sc[:, r0:r0 + chunk] * correction_factor + jnp.sum(weights, axis=0, keepdims=True)
            m_sc[:, r0:r0 + chunk] = new_max
            c_sc[:, r0:r0 + chunk] = correction_factor
            p_sc[:, r0:r0 + chunk] = weights.astype(jnp.bfloat16)
        acc_sc[...] = acc_sc[...] * c_sc[...] + lax.dot_general(kv_ref[kb, 1], p_sc[...], (((0,), (0,)), ((), ())), preferred_element_type=jnp.float32)

    def body(kb, carry):
        run_block(kb, False)
        return carry
    lax.fori_loop(0, position, body, 0)
    run_block(position, True)
    o_ref[...] = (acc_sc[...] / l_sc[...]).astype(o_ref.dtype)


def causal_attention(position, queries, gathered_kv, chunk=256):
    blocks, _, tok_rows, width = gathered_kv.shape
    heads = queries.shape[1] // width
    rows = heads * tok_rows
    queries_t = queries.reshape(tok_rows, heads, width).transpose(2, 1, 0).reshape(width, rows)
    kernel = functools.partial(attend_kernel, tok=tok_rows, width=width, chunk=chunk)
    out_t = pl.pallas_call(
        kernel,
        in_specs=[pl.BlockSpec(memory_space=pltpu.SMEM)] + [pl.BlockSpec(memory_space=pltpu.VMEM)] * 2,
        out_specs=pl.BlockSpec(memory_space=pltpu.VMEM),
        out_shape=jax.ShapeDtypeStruct((width, rows), queries.dtype),
        scratch_shapes=[
            pltpu.VMEM((tok_rows, rows), jnp.bfloat16),
            pltpu.VMEM((1, rows), jnp.float32),
            pltpu.VMEM((1, rows), jnp.float32),
            pltpu.VMEM((1, rows), jnp.float32),
            pltpu.VMEM((width, rows), jnp.float32),
        ],
    )(position.reshape(1), queries_t, gathered_kv)
    return out_t.reshape(width, heads, tok_rows).transpose(2, 1, 0).reshape(tok_rows, heads * width)


def shifted(block, axis, distance):
    devices = range(lax.axis_size(axis))
    route = [(i - distance, i) for i in devices if i - distance in devices]
    return lax.ppermute(block, axis, route)


def summed_over(part, axis):
    count = lax.axis_size(axis)
    total = part
    distance = 1
    while distance < count:
        route = [(i, i ^ distance) for i in range(count)]
        total = total + lax.ppermute(total, axis, route)
        distance *= 2
    return total


def packed(state, log_span):
    heads = log_span.shape[-1]
    lanes = state.shape[-1]
    rows = state.astype(jnp.bfloat16).reshape(state.shape[0], -1, lanes)
    high = lax.reduce_precision(log_span, exponent_bits=8, mantissa_bits=7)
    rest = log_span - high
    middle = lax.reduce_precision(rest, exponent_bits=8, mantissa_bits=7)
    low = rest - middle
    parts = jnp.stack((high, middle, low), axis=1).astype(jnp.bfloat16)
    tail = jnp.pad(parts, ((0, 0), (0, 16 - parts.shape[1]), (0, lanes - heads)))
    return jnp.concatenate((rows, tail), axis=1)


def unpacked(block, state_shape):
    heads = state_shape[1]
    body_rows = block.shape[1] - 16
    state = block[:, :body_rows].reshape(state_shape).astype(jnp.float32)
    parts = block[:, body_rows:body_rows + 3, :heads].astype(jnp.float32)
    return state, (parts[:, 0] + parts[:, 1]) + parts[:, 2]


def carried_scan(local_state, block_log_decay, axis, count):
    sent = packed(local_state, block_log_decay)
    one_back_state, one_back_decay = unpacked(shifted(sent, axis, 1), local_state.shape)
    two_back_state, two_back_decay = unpacked(shifted(sent, axis, 2), local_state.shape)
    state = jnp.exp(one_back_decay)[..., None, None] * two_back_state + one_back_state
    log_span = one_back_decay + two_back_decay
    distance = 2
    while distance < count:
        earlier_state, earlier_span = unpacked(
            shifted(packed(state, log_span), axis, distance), local_state.shape
        )
        state = jnp.exp(log_span)[..., None, None] * earlier_state + state
        log_span = log_span + earlier_span
        distance *= 2
    return state


def chip_carried_scan(local_state, block_log_decay):
    core = lax.axis_index("core")
    swap = [(0, 1), (1, 0)]
    sent = packed(local_state, block_log_decay)
    own_state, own_decay = unpacked(sent, local_state.shape)
    mate_state, mate_decay = unpacked(lax.ppermute(sent, "core", swap), local_state.shape)
    first_state = jnp.where(core == 0, own_state, mate_state)
    first_decay = jnp.where(core == 0, own_decay, mate_decay)
    second_state = jnp.where(core == 0, mate_state, own_state)
    second_decay = jnp.where(core == 0, mate_decay, own_decay)
    chip_state = jnp.exp(second_decay)[..., None, None] * first_state + second_state
    chip_decay = first_decay + second_decay
    half = local_state.shape[1] // 2
    chip_prefix = carried_scan(
        lax.dynamic_slice_in_dim(chip_state, core * half, half, axis=1),
        lax.dynamic_slice_in_dim(chip_decay, core * half, half, axis=1),
        "chip",
        lax.axis_size("chip"),
    )
    other_prefix = lax.ppermute(chip_prefix.astype(jnp.bfloat16), "core", swap).astype(jnp.float32)
    prefix = jnp.where(
        core == 0,
        jnp.concatenate((chip_prefix, other_prefix), axis=1),
        jnp.concatenate((other_prefix, chip_prefix), axis=1),
    )
    return jnp.where(
        core == 0, prefix, jnp.exp(first_decay)[..., None, None] * prefix + first_state
    )


def local(
    queries,
    key_rows,
    value_head_rows,
    ssm_input,
    gate_input,
    b_matrix,
    c_matrix,
    step_size,
    log_decay,
    skip_gain,
    norm_gain,
):
    tok_rows = queries.shape[0]
    position = lax.axis_index(CTX)

    gathered_kv = lax.all_gather(jnp.stack((key_rows, value_head_rows)), CTX)

    heads_local = step_size.shape[0]
    groups_local = b_matrix.shape[1] // N
    heads_group = heads_local // groups_local
    mixer_in = ssm_input.reshape(tok_rows, groups_local, heads_group, P_SIZE)
    in_maps = b_matrix.reshape(tok_rows, groups_local, N)
    out_maps = c_matrix.reshape(tok_rows, groups_local, N)
    steps_here = step_size.reshape(groups_local, heads_group, tok_rows)
    cumul = jnp.cumsum(log_decay.reshape(groups_local, heads_group, tok_rows), axis=-1)
    causal = jnp.tril(jnp.ones((tok_rows, tok_rows), dtype=bool))
    gram = jnp.einsum("tgn,sgn->gts", out_maps, in_maps, preferred_element_type=jnp.float32)
    spread = jnp.where(causal, cumul[..., :, None] - cumul[..., None, :], 0.0)
    mixing = jnp.where(
        causal, gram[:, None] * jnp.exp(spread) * steps_here[..., None, :], 0.0
    ).astype(jnp.bfloat16)
    inner = jnp.einsum("ghts,sghp->tghp", mixing, mixer_in, preferred_element_type=jnp.float32)
    weight_end = jnp.exp(cumul[..., -1:] - cumul) * steps_here
    weighted = (mixer_in * weight_end.transpose(2, 0, 1)[..., None]).astype(jnp.bfloat16)
    local_state = jnp.einsum(
        "sghp,sgn->ghpn", weighted, in_maps, preferred_element_type=jnp.float32
    )
    block_log_decay = cumul[..., -1]

    incoming = chip_carried_scan(local_state, block_log_decay)

    attention_out = causal_attention(position, queries, gathered_kv)

    carried_out = jnp.einsum(
        "ghpn,tgn->tghp", incoming, out_maps.astype(jnp.float32), precision=lax.Precision.HIGHEST
    )
    carried_out = carried_out * jnp.exp(cumul).transpose(2, 0, 1)[..., None]
    direct = skip_gain.reshape(groups_local, heads_group)[None, :, :, None] * mixer_in.astype(
        jnp.float32
    )
    outputs = (inner + carried_out + direct).reshape(tok_rows, -1)
    gated = outputs * jax.nn.silu(gate_input.astype(jnp.float32))
    square_total = summed_over(jnp.sum(gated * gated, axis=-1), "tp")
    scaling = lax.rsqrt(square_total / (STATE_HEADS * P_SIZE) + 1e-05)
    mixer_out = (gated * scaling[:, None] * norm_gain.astype(jnp.float32)).astype(jnp.bfloat16)
    return (attention_out, mixer_out)


def solution(mesh):
    placed = (
        P("ctx", "tp"),
        P("ctx", "tp"),
        P("ctx", "tp"),
        P("ctx", "tp"),
        P("ctx", "tp"),
        P("ctx", "tp"),
        P("ctx", "tp"),
        P("tp", "ctx"),
        P("tp", "ctx"),
        P("tp"),
        P("tp"),
    )
    fine_mesh = jax.sharding.Mesh(
        mesh.devices.reshape(mesh.shape["ctx"] // 2, 2, mesh.shape["tp"]), CTX + ("tp",)
    )
    placed = tuple(P(*[CTX if axis == "ctx" else axis for axis in spec]) for spec in placed)
    return jax.shard_map(
        local,
        mesh=fine_mesh,
        in_specs=placed,
        out_specs=(P(CTX, "tp"), P(CTX, "tp")),
        check_vma=False,
    )
```

```python
import functools

import jax
import jax.numpy as jnp
from jax import lax
from jax.experimental import pallas as pl
from jax.experimental.pallas import tpu as pltpu
from jax.sharding import PartitionSpec as P

HEAD_WIDTH = 128
STATE_HEADS = 128
P_SIZE = 64
N = 128


causal_score = -1e30
CTX = ("chip", "core")


def attend_kernel(pos_ref, qt_ref, kv_ref, o_ref, p_sc, p2_sc, m_sc, l_sc, c_sc, acc_sc, *, tok, width, chunk):
    position = pos_ref[0]
    score_factor = width ** (-0.5) * 1.4426950408889634
    rows = qt_ref.shape[1]
    block_rows = kv_ref.shape[2]
    m_sc[...] = jnp.full(m_sc.shape, causal_score, jnp.float32)
    l_sc[...] = jnp.zeros(l_sc.shape, jnp.float32)
    acc_sc[...] = jnp.zeros(acc_sc.shape, jnp.float32)

    def run_block(kb, masked):
        key_portion = kv_ref[kb, 0]
        for c in range(rows // chunk):
            r0 = c * chunk
            score_t = jnp.dot(key_portion, qt_ref[:, r0:r0 + chunk],
                              preferred_element_type=jnp.float32)
            if masked:
                key_idx = lax.broadcasted_iota(jnp.int32, (block_rows, chunk), 0)
                query_idx = (r0 % tok) + lax.broadcasted_iota(jnp.int32, (block_rows, chunk), 1)
                is_valid = key_idx <= query_idx
                score_t = jnp.where(is_valid, score_t, causal_score)
            run_max = m_sc[:, r0:r0 + chunk]
            new_max = jnp.maximum(run_max, jnp.max(score_t, axis=0, keepdims=True))
            weights = jnp.exp2(score_t * score_factor - new_max * score_factor)
            if masked:
                weights = jnp.where(is_valid, weights, 0.0)
            correction_factor = jnp.exp2((run_max - new_max) * score_factor)
            l_sc[:, r0:r0 + chunk] = l_sc[:, r0:r0 + chunk] * correction_factor + jnp.sum(weights, axis=0, keepdims=True)
            m_sc[:, r0:r0 + chunk] = new_max
            c_sc[:, r0:r0 + chunk] = correction_factor
            p_sc[:, r0:r0 + chunk] = weights.astype(jnp.bfloat16)
        acc_sc[...] = acc_sc[...] * c_sc[...] + lax.dot_general(kv_ref[kb, 1], p_sc[...], (((0,), (0,)), ((), ())), preferred_element_type=jnp.float32)

    def run_pair(kb):
        keys = (kv_ref[kb, 0], kv_ref[kb + 1, 0])
        for c in range(rows // chunk):
            r0 = c * chunk
            scores = [jnp.dot(k, qt_ref[:, r0:r0 + chunk], preferred_element_type=jnp.float32) for k in keys]
            run_max = m_sc[:, r0:r0 + chunk]
            block_max = jnp.maximum(jnp.max(scores[0], axis=0, keepdims=True), jnp.max(scores[1], axis=0, keepdims=True))
            new_max = jnp.maximum(run_max, block_max)
            weights = [jnp.exp2(s * score_factor - new_max * score_factor) for s in scores]
            correction_factor = jnp.exp2((run_max - new_max) * score_factor)
            l_sc[:, r0:r0 + chunk] = l_sc[:, r0:r0 + chunk] * correction_factor + (
                jnp.sum(weights[0], axis=0, keepdims=True) + jnp.sum(weights[1], axis=0, keepdims=True))
            m_sc[:, r0:r0 + chunk] = new_max
            c_sc[:, r0:r0 + chunk] = correction_factor
            p_sc[:, r0:r0 + chunk] = weights[0].astype(jnp.bfloat16)
            p2_sc[:, r0:r0 + chunk] = weights[1].astype(jnp.bfloat16)
        acc_sc[...] = acc_sc[...] * c_sc[...] + (
            lax.dot_general(kv_ref[kb, 1], p_sc[...], (((0,), (0,)), ((), ())), preferred_element_type=jnp.float32)
            + lax.dot_general(kv_ref[kb + 1, 1], p2_sc[...], (((0,), (0,)), ((), ())), preferred_element_type=jnp.float32))

    def pair_body(i, carry):
        run_pair(2 * i)
        return carry
    lax.fori_loop(0, position // 2, pair_body, 0)

    @pl.when(lax.rem(position, 2) == 1)
    def _odd():
        run_block(position - 1, False)

    run_block(position, True)
    o_ref[...] = (acc_sc[...] / l_sc[...]).astype(o_ref.dtype)


def causal_attention(position, queries, gathered_kv, chunk=256):
    blocks, _, tok_rows, width = gathered_kv.shape
    heads = queries.shape[1] // width
    rows = heads * tok_rows
    queries_t = queries.reshape(tok_rows, heads, width).transpose(2, 1, 0).reshape(width, rows)
    kernel = functools.partial(attend_kernel, tok=tok_rows, width=width, chunk=chunk)
    out_t = pl.pallas_call(
        kernel,
        in_specs=[pl.BlockSpec(memory_space=pltpu.SMEM)] + [pl.BlockSpec(memory_space=pltpu.VMEM)] * 2,
        out_specs=pl.BlockSpec(memory_space=pltpu.VMEM),
        out_shape=jax.ShapeDtypeStruct((width, rows), queries.dtype),
        scratch_shapes=[
            pltpu.VMEM((tok_rows, rows), jnp.bfloat16),
            pltpu.VMEM((tok_rows, rows), jnp.bfloat16),
            pltpu.VMEM((1, rows), jnp.float32),
            pltpu.VMEM((1, rows), jnp.float32),
            pltpu.VMEM((1, rows), jnp.float32),
            pltpu.VMEM((width, rows), jnp.float32),
        ],
    )(position.reshape(1), queries_t, gathered_kv)
    return out_t.reshape(width, heads, tok_rows).transpose(2, 1, 0).reshape(tok_rows, heads * width)


def shifted(block, axis, distance):
    devices = range(lax.axis_size(axis))
    route = [(i - distance, i) for i in devices if i - distance in devices]
    return lax.ppermute(block, axis, route)


def summed_over(part, axis):
    count = lax.axis_size(axis)
    total = part
    distance = 1
    while distance < count:
        route = [(i, i ^ distance) for i in range(count)]
        total = total + lax.ppermute(total, axis, route)
        distance *= 2
    return total


def packed(state, log_span):
    heads = log_span.shape[-1]
    lanes = state.shape[-1]
    rows = state.astype(jnp.bfloat16).reshape(state.shape[0], -1, lanes)
    high = lax.reduce_precision(log_span, exponent_bits=8, mantissa_bits=7)
    rest = log_span - high
    middle = lax.reduce_precision(rest, exponent_bits=8, mantissa_bits=7)
    low = rest - middle
    parts = jnp.stack((high, middle, low), axis=1).astype(jnp.bfloat16)
    tail = jnp.pad(parts, ((0, 0), (0, 16 - parts.shape[1]), (0, lanes - heads)))
    return jnp.concatenate((rows, tail), axis=1)


def unpacked(block, state_shape):
    heads = state_shape[1]
    body_rows = block.shape[1] - 16
    state = block[:, :body_rows].reshape(state_shape).astype(jnp.float32)
    parts = block[:, body_rows:body_rows + 3, :heads].astype(jnp.float32)
    return state, (parts[:, 0] + parts[:, 1]) + parts[:, 2]


def carried_scan(local_state, block_log_decay, axis, count):
    sent = packed(local_state, block_log_decay)
    one_back_state, one_back_decay = unpacked(shifted(sent, axis, 1), local_state.shape)
    two_back_state, two_back_decay = unpacked(shifted(sent, axis, 2), local_state.shape)
    state = jnp.exp(one_back_decay)[..., None, None] * two_back_state + one_back_state
    log_span = one_back_decay + two_back_decay
    distance = 2
    while distance < count:
        earlier_state, earlier_span = unpacked(
            shifted(packed(state, log_span), axis, distance), local_state.shape
        )
        state = jnp.exp(log_span)[..., None, None] * earlier_state + state
        log_span = log_span + earlier_span
        distance *= 2
    return state


def chip_carried_scan(local_state, block_log_decay):
    core = lax.axis_index("core")
    swap = [(0, 1), (1, 0)]
    sent = packed(local_state, block_log_decay)
    own_state, own_decay = unpacked(sent, local_state.shape)
    mate_state, mate_decay = unpacked(lax.ppermute(sent, "core", swap), local_state.shape)
    first_state = jnp.where(core == 0, own_state, mate_state)
    first_decay = jnp.where(core == 0, own_decay, mate_decay)
    second_state = jnp.where(core == 0, mate_state, own_state)
    second_decay = jnp.where(core == 0, mate_decay, own_decay)
    chip_state = jnp.exp(second_decay)[..., None, None] * first_state + second_state
    chip_decay = first_decay + second_decay
    half = local_state.shape[1] // 2
    chip_prefix = carried_scan(
        lax.dynamic_slice_in_dim(chip_state, core * half, half, axis=1),
        lax.dynamic_slice_in_dim(chip_decay, core * half, half, axis=1),
        "chip",
        lax.axis_size("chip"),
    )
    other_prefix = lax.ppermute(chip_prefix.astype(jnp.bfloat16), "core", swap).astype(jnp.float32)
    prefix = jnp.where(
        core == 0,
        jnp.concatenate((chip_prefix, other_prefix), axis=1),
        jnp.concatenate((other_prefix, chip_prefix), axis=1),
    )
    return jnp.where(
        core == 0, prefix, jnp.exp(first_decay)[..., None, None] * prefix + first_state
    )


def local(
    queries,
    key_rows,
    value_head_rows,
    ssm_input,
    gate_input,
    b_matrix,
    c_matrix,
    step_size,
    log_decay,
    skip_gain,
    norm_gain,
):
    tok_rows = queries.shape[0]
    position = lax.axis_index(CTX)

    gathered_kv = lax.all_gather(jnp.stack((key_rows, value_head_rows)), CTX)

    heads_local = step_size.shape[0]
    groups_local = b_matrix.shape[1] // N
    heads_group = heads_local // groups_local
    mixer_in = ssm_input.reshape(tok_rows, groups_local, heads_group, P_SIZE)
    in_maps = b_matrix.reshape(tok_rows, groups_local, N)
    out_maps = c_matrix.reshape(tok_rows, groups_local, N)
    steps_here = step_size.reshape(groups_local, heads_group, tok_rows)
    cumul = jnp.cumsum(log_decay.reshape(groups_local, heads_group, tok_rows), axis=-1)
    causal = jnp.tril(jnp.ones((tok_rows, tok_rows), dtype=bool))
    gram = jnp.einsum("tgn,sgn->gts", out_maps, in_maps, preferred_element_type=jnp.float32)
    spread = jnp.where(causal, cumul[..., :, None] - cumul[..., None, :], 0.0)
    mixing = jnp.where(
        causal, gram[:, None] * jnp.exp(spread) * steps_here[..., None, :], 0.0
    ).astype(jnp.bfloat16)
    inner = jnp.einsum("ghts,sghp->tghp", mixing, mixer_in, preferred_element_type=jnp.float32)
    weight_end = jnp.exp(cumul[..., -1:] - cumul) * steps_here
    weighted = (mixer_in * weight_end.transpose(2, 0, 1)[..., None]).astype(jnp.bfloat16)
    local_state = jnp.einsum(
        "sghp,sgn->ghpn", weighted, in_maps, preferred_element_type=jnp.float32
    )
    block_log_decay = cumul[..., -1]

    incoming = chip_carried_scan(local_state, block_log_decay)

    attention_out = causal_attention(position, queries, gathered_kv)

    carried_out = jnp.einsum(
        "ghpn,tgn->tghp", incoming, out_maps.astype(jnp.float32), precision=lax.Precision.HIGHEST
    )
    carried_out = carried_out * jnp.exp(cumul).transpose(2, 0, 1)[..., None]
    direct = skip_gain.reshape(groups_local, heads_group)[None, :, :, None] * mixer_in.astype(
        jnp.float32
    )
    outputs = (inner + carried_out + direct).reshape(tok_rows, -1)
    gated = outputs * jax.nn.silu(gate_input.astype(jnp.float32))
    square_total = summed_over(jnp.sum(gated * gated, axis=-1), "tp")
    scaling = lax.rsqrt(square_total / (STATE_HEADS * P_SIZE) + 1e-05)
    mixer_out = (gated * scaling[:, None] * norm_gain.astype(jnp.float32)).astype(jnp.bfloat16)
    return (attention_out, mixer_out)


def solution(mesh):
    placed = (
        P("ctx", "tp"),
        P("ctx", "tp"),
        P("ctx", "tp"),
        P("ctx", "tp"),
        P("ctx", "tp"),
        P("ctx", "tp"),
        P("ctx", "tp"),
        P("tp", "ctx"),
        P("tp", "ctx"),
        P("tp"),
        P("tp"),
    )
    fine_mesh = jax.sharding.Mesh(
        mesh.devices.reshape(mesh.shape["ctx"] // 2, 2, mesh.shape["tp"]), CTX + ("tp",)
    )
    placed = tuple(P(*[CTX if axis == "ctx" else axis for axis in spec]) for spec in placed)
    return jax.shard_map(
        local,
        mesh=fine_mesh,
        in_specs=placed,
        out_specs=(P(CTX, "tp"), P(CTX, "tp")),
        check_vma=False,
    )
```

```python
import functools

import jax
import jax.numpy as jnp
from jax import lax
from jax.experimental import pallas as pl
from jax.experimental.pallas import tpu as pltpu
from jax.sharding import PartitionSpec as P

HEAD_WIDTH = 128
STATE_HEADS = 128
P_SIZE = 64
N = 128


causal_score = -1e30
CTX = ("chip", "core")


def attend_kernel(pos_ref, qt_ref, kv_ref, o_ref, p_sc, p2_sc, m_sc, l_sc, c_sc, acc_sc, *, tok, width, chunk):
    position = pos_ref[0]
    score_factor = width ** (-0.5) * 1.4426950408889634
    rows = qt_ref.shape[1]
    block_rows = kv_ref.shape[2]
    m_sc[...] = jnp.full(m_sc.shape, causal_score, jnp.float32)
    l_sc[...] = jnp.zeros(l_sc.shape, jnp.float32)
    acc_sc[...] = jnp.zeros(acc_sc.shape, jnp.float32)

    def run_block(kb, masked):
        key_portion = kv_ref[kb, 0]
        for c in range(rows // chunk):
            r0 = c * chunk
            score_t = jnp.dot(key_portion, qt_ref[:, r0:r0 + chunk],
                              preferred_element_type=jnp.float32)
            if masked:
                key_idx = lax.broadcasted_iota(jnp.int32, (block_rows, chunk), 0)
                query_idx = (r0 % tok) + lax.broadcasted_iota(jnp.int32, (block_rows, chunk), 1)
                is_valid = key_idx <= query_idx
                score_t = jnp.where(is_valid, score_t, causal_score)
            run_max = m_sc[:, r0:r0 + chunk]
            new_max = jnp.maximum(run_max, jnp.max(score_t, axis=0, keepdims=True))
            weights = jnp.exp2(score_t * score_factor - new_max * score_factor)
            if masked:
                weights = jnp.where(is_valid, weights, 0.0)
            correction_factor = jnp.exp2((run_max - new_max) * score_factor)
            l_sc[:, r0:r0 + chunk] = l_sc[:, r0:r0 + chunk] * correction_factor + jnp.sum(weights, axis=0, keepdims=True)
            m_sc[:, r0:r0 + chunk] = new_max
            c_sc[:, r0:r0 + chunk] = correction_factor
            p_sc[:, r0:r0 + chunk] = weights.astype(jnp.bfloat16)
        acc_sc[...] = acc_sc[...] * c_sc[...] + lax.dot_general(kv_ref[kb, 1], p_sc[...], (((0,), (0,)), ((), ())), preferred_element_type=jnp.float32)

    def run_pair(kb):
        keys = (kv_ref[kb, 0], kv_ref[kb + 1, 0])
        for c in range(rows // chunk):
            r0 = c * chunk
            scores = [jnp.dot(k, qt_ref[:, r0:r0 + chunk], preferred_element_type=jnp.float32) for k in keys]
            run_max = m_sc[:, r0:r0 + chunk]
            block_max = jnp.maximum(jnp.max(scores[0], axis=0, keepdims=True), jnp.max(scores[1], axis=0, keepdims=True))
            new_max = jnp.maximum(run_max, block_max)
            weights = [jnp.exp2(s * score_factor - new_max * score_factor) for s in scores]
            correction_factor = jnp.exp2((run_max - new_max) * score_factor)
            l_sc[:, r0:r0 + chunk] = l_sc[:, r0:r0 + chunk] * correction_factor + (
                jnp.sum(weights[0], axis=0, keepdims=True) + jnp.sum(weights[1], axis=0, keepdims=True))
            m_sc[:, r0:r0 + chunk] = new_max
            c_sc[:, r0:r0 + chunk] = correction_factor
            p_sc[:, r0:r0 + chunk] = weights[0].astype(jnp.bfloat16)
            p2_sc[:, r0:r0 + chunk] = weights[1].astype(jnp.bfloat16)
        acc_sc[...] = acc_sc[...] * c_sc[...] + (
            lax.dot_general(kv_ref[kb, 1], p_sc[...], (((0,), (0,)), ((), ())), preferred_element_type=jnp.float32)
            + lax.dot_general(kv_ref[kb + 1, 1], p2_sc[...], (((0,), (0,)), ((), ())), preferred_element_type=jnp.float32))

    def pair_body(i, carry):
        run_pair(2 * i)
        return carry
    lax.fori_loop(0, position // 2, pair_body, 0)

    @pl.when(lax.rem(position, 2) == 1)
    def _odd():
        run_block(position - 1, False)

    run_block(position, True)
    for h in range(rows // tok):
        columns = slice(h * tok, (h + 1) * tok)
        o_ref[:, h * width:(h + 1) * width] = (acc_sc[:, columns] / l_sc[:, columns]).T.astype(o_ref.dtype)


def causal_attention(position, queries, gathered_kv, chunk=256):
    blocks, _, tok_rows, width = gathered_kv.shape
    heads = queries.shape[1] // width
    rows = heads * tok_rows
    queries_t = queries.reshape(tok_rows, heads, width).transpose(2, 1, 0).reshape(width, rows)
    kernel = functools.partial(attend_kernel, tok=tok_rows, width=width, chunk=chunk)
    return pl.pallas_call(
        kernel,
        in_specs=[pl.BlockSpec(memory_space=pltpu.SMEM)] + [pl.BlockSpec(memory_space=pltpu.VMEM)] * 2,
        out_specs=pl.BlockSpec(memory_space=pltpu.VMEM),
        out_shape=jax.ShapeDtypeStruct(queries.shape, queries.dtype),
        scratch_shapes=[
            pltpu.VMEM((tok_rows, rows), jnp.bfloat16),
            pltpu.VMEM((tok_rows, rows), jnp.bfloat16),
            pltpu.VMEM((1, rows), jnp.float32),
            pltpu.VMEM((1, rows), jnp.float32),
            pltpu.VMEM((1, rows), jnp.float32),
            pltpu.VMEM((width, rows), jnp.float32),
        ],
    )(position.reshape(1), queries_t, gathered_kv)


def shifted(block, axis, distance):
    devices = range(lax.axis_size(axis))
    route = [(i - distance, i) for i in devices if i - distance in devices]
    return lax.ppermute(block, axis, route)


def summed_over(part, axis):
    count = lax.axis_size(axis)
    total = part
    distance = 1
    while distance < count:
        route = [(i, i ^ distance) for i in range(count)]
        total = total + lax.ppermute(total, axis, route)
        distance *= 2
    return total


def packed(state, log_span):
    heads = log_span.shape[-1]
    lanes = state.shape[-1]
    rows = state.astype(jnp.bfloat16).reshape(state.shape[0], -1, lanes)
    high = lax.reduce_precision(log_span, exponent_bits=8, mantissa_bits=7)
    rest = log_span - high
    middle = lax.reduce_precision(rest, exponent_bits=8, mantissa_bits=7)
    low = rest - middle
    parts = jnp.stack((high, middle, low), axis=1).astype(jnp.bfloat16)
    tail = jnp.pad(parts, ((0, 0), (0, 16 - parts.shape[1]), (0, lanes - heads)))
    return jnp.concatenate((rows, tail), axis=1)


def unpacked(block, state_shape):
    heads = state_shape[1]
    body_rows = block.shape[1] - 16
    state = block[:, :body_rows].reshape(state_shape).astype(jnp.float32)
    parts = block[:, body_rows:body_rows + 3, :heads].astype(jnp.float32)
    return state, (parts[:, 0] + parts[:, 1]) + parts[:, 2]


def carried_scan(local_state, block_log_decay, axis, count):
    sent = packed(local_state, block_log_decay)
    one_back_state, one_back_decay = unpacked(shifted(sent, axis, 1), local_state.shape)
    two_back_state, two_back_decay = unpacked(shifted(sent, axis, 2), local_state.shape)
    state = jnp.exp(one_back_decay)[..., None, None] * two_back_state + one_back_state
    log_span = one_back_decay + two_back_decay
    distance = 2
    while distance < count:
        earlier_state, earlier_span = unpacked(
            shifted(packed(state, log_span), axis, distance), local_state.shape
        )
        state = jnp.exp(log_span)[..., None, None] * earlier_state + state
        log_span = log_span + earlier_span
        distance *= 2
    return state


def chip_carried_scan(local_state, block_log_decay):
    core = lax.axis_index("core")
    swap = [(0, 1), (1, 0)]
    sent = packed(local_state, block_log_decay)
    own_state, own_decay = unpacked(sent, local_state.shape)
    mate_state, mate_decay = unpacked(lax.ppermute(sent, "core", swap), local_state.shape)
    first_state = jnp.where(core == 0, own_state, mate_state)
    first_decay = jnp.where(core == 0, own_decay, mate_decay)
    second_state = jnp.where(core == 0, mate_state, own_state)
    second_decay = jnp.where(core == 0, mate_decay, own_decay)
    chip_state = jnp.exp(second_decay)[..., None, None] * first_state + second_state
    chip_decay = first_decay + second_decay
    half = local_state.shape[1] // 2
    chip_prefix = carried_scan(
        lax.dynamic_slice_in_dim(chip_state, core * half, half, axis=1),
        lax.dynamic_slice_in_dim(chip_decay, core * half, half, axis=1),
        "chip",
        lax.axis_size("chip"),
    )
    other_prefix = lax.ppermute(chip_prefix.astype(jnp.bfloat16), "core", swap).astype(jnp.float32)
    prefix = jnp.where(
        core == 0,
        jnp.concatenate((chip_prefix, other_prefix), axis=1),
        jnp.concatenate((other_prefix, chip_prefix), axis=1),
    )
    return jnp.where(
        core == 0, prefix, jnp.exp(first_decay)[..., None, None] * prefix + first_state
    )


def local(
    queries,
    key_rows,
    value_head_rows,
    ssm_input,
    gate_input,
    b_matrix,
    c_matrix,
    step_size,
    log_decay,
    skip_gain,
    norm_gain,
):
    tok_rows = queries.shape[0]
    position = lax.axis_index(CTX)

    gathered_kv = lax.all_gather(jnp.stack((key_rows, value_head_rows)), CTX)

    heads_local = step_size.shape[0]
    groups_local = b_matrix.shape[1] // N
    heads_group = heads_local // groups_local
    mixer_in = ssm_input.reshape(tok_rows, groups_local, heads_group, P_SIZE)
    in_maps = b_matrix.reshape(tok_rows, groups_local, N)
    out_maps = c_matrix.reshape(tok_rows, groups_local, N)
    steps_here = step_size.reshape(groups_local, heads_group, tok_rows)
    cumul = jnp.cumsum(log_decay.reshape(groups_local, heads_group, tok_rows), axis=-1)
    causal = jnp.tril(jnp.ones((tok_rows, tok_rows), dtype=bool))
    gram = jnp.einsum("tgn,sgn->gts", out_maps, in_maps, preferred_element_type=jnp.float32)
    spread = jnp.where(causal, cumul[..., :, None] - cumul[..., None, :], 0.0)
    mixing = jnp.where(
        causal, gram[:, None] * jnp.exp(spread) * steps_here[..., None, :], 0.0
    ).astype(jnp.bfloat16)
    inner = jnp.einsum("ghts,sghp->tghp", mixing, mixer_in, preferred_element_type=jnp.float32)
    weight_end = jnp.exp(cumul[..., -1:] - cumul) * steps_here
    weighted = (mixer_in * weight_end.transpose(2, 0, 1)[..., None]).astype(jnp.bfloat16)
    local_state = jnp.einsum(
        "sghp,sgn->ghpn", weighted, in_maps, preferred_element_type=jnp.float32
    )
    block_log_decay = cumul[..., -1]

    incoming = chip_carried_scan(local_state, block_log_decay)

    attention_out = causal_attention(position, queries, gathered_kv)

    carried_out = jnp.einsum(
        "ghpn,tgn->tghp", incoming, out_maps.astype(jnp.float32), precision=lax.Precision.HIGHEST
    )
    carried_out = carried_out * jnp.exp(cumul).transpose(2, 0, 1)[..., None]
    direct = skip_gain.reshape(groups_local, heads_group)[None, :, :, None] * mixer_in.astype(
        jnp.float32
    )
    outputs = (inner + carried_out + direct).reshape(tok_rows, -1)
    gated = outputs * jax.nn.silu(gate_input.astype(jnp.float32))
    square_total = summed_over(jnp.sum(gated * gated, axis=-1), "tp")
    scaling = lax.rsqrt(square_total / (STATE_HEADS * P_SIZE) + 1e-05)
    mixer_out = (gated * scaling[:, None] * norm_gain.astype(jnp.float32)).astype(jnp.bfloat16)
    return (attention_out, mixer_out)


def solution(mesh):
    placed = (
        P("ctx", "tp"),
        P("ctx", "tp"),
        P("ctx", "tp"),
        P("ctx", "tp"),
        P("ctx", "tp"),
        P("ctx", "tp"),
        P("ctx", "tp"),
        P("tp", "ctx"),
        P("tp", "ctx"),
        P("tp"),
        P("tp"),
    )
    fine_mesh = jax.sharding.Mesh(
        mesh.devices.reshape(mesh.shape["ctx"] // 2, 2, mesh.shape["tp"]), CTX + ("tp",)
    )
    placed = tuple(P(*[CTX if axis == "ctx" else axis for axis in spec]) for spec in placed)
    return jax.shard_map(
        local,
        mesh=fine_mesh,
        in_specs=placed,
        out_specs=(P(CTX, "tp"), P(CTX, "tp")),
        check_vma=False,
    )
```

```python
import functools

import jax
import jax.numpy as jnp
from jax import lax
from jax.experimental import pallas as pl
from jax.experimental.pallas import tpu as pltpu
from jax.sharding import PartitionSpec as P

HEAD_WIDTH = 128
STATE_HEADS = 128
P_SIZE = 64
N = 128


causal_score = -1e30
CTX = ("chip", "core")


def attend_kernel(pos_ref, qt_ref, kv_ref, o_ref, p_sc, p2_sc, m_sc, l_sc, c_sc, acc_sc, *, tok, width, chunk):
    position = pos_ref[0]
    score_factor = width ** (-0.5) * 1.4426950408889634
    rows = qt_ref.shape[1]
    block_rows = kv_ref.shape[2]
    m_sc[...] = jnp.full(m_sc.shape, causal_score, jnp.float32)
    l_sc[...] = jnp.zeros(l_sc.shape, jnp.float32)
    acc_sc[...] = jnp.zeros(acc_sc.shape, jnp.float32)

    def run_block(kb, masked):
        key_portion = kv_ref[kb, 0]
        for c in range(rows // chunk):
            r0 = c * chunk
            score_t = jnp.dot(key_portion, qt_ref[:, r0:r0 + chunk],
                              preferred_element_type=jnp.float32)
            if masked:
                key_idx = lax.broadcasted_iota(jnp.int32, (block_rows, chunk), 0)
                query_idx = (r0 % tok) + lax.broadcasted_iota(jnp.int32, (block_rows, chunk), 1)
                is_valid = key_idx <= query_idx
                score_t = jnp.where(is_valid, score_t, causal_score)
            run_max = m_sc[:, r0:r0 + chunk]
            new_max = jnp.maximum(run_max, jnp.max(score_t, axis=0, keepdims=True))
            weights = jnp.exp2(score_t * score_factor - new_max * score_factor)
            if masked:
                weights = jnp.where(is_valid, weights, 0.0)
            correction_factor = jnp.exp2((run_max - new_max) * score_factor)
            l_sc[:, r0:r0 + chunk] = l_sc[:, r0:r0 + chunk] * correction_factor + jnp.sum(weights, axis=0, keepdims=True)
            m_sc[:, r0:r0 + chunk] = new_max
            c_sc[:, r0:r0 + chunk] = correction_factor
            p_sc[:, r0:r0 + chunk] = weights.astype(jnp.bfloat16)
        acc_sc[...] = acc_sc[...] * c_sc[...] + lax.dot_general(kv_ref[kb, 1], p_sc[...], (((0,), (0,)), ((), ())), preferred_element_type=jnp.float32)

    def run_pair(kb, masked=False):
        keys = (kv_ref[kb, 0], kv_ref[kb + 1, 0])
        for c in range(rows // chunk):
            r0 = c * chunk
            scores = [jnp.dot(k, qt_ref[:, r0:r0 + chunk], preferred_element_type=jnp.float32) for k in keys]
            if masked:
                key_idx = lax.broadcasted_iota(jnp.int32, (block_rows, chunk), 0)
                query_idx = (r0 % tok) + lax.broadcasted_iota(jnp.int32, (block_rows, chunk), 1)
                is_valid = key_idx <= query_idx
                scores[1] = jnp.where(is_valid, scores[1], causal_score)
            run_max = m_sc[:, r0:r0 + chunk]
            block_max = jnp.maximum(jnp.max(scores[0], axis=0, keepdims=True), jnp.max(scores[1], axis=0, keepdims=True))
            new_max = jnp.maximum(run_max, block_max)
            weights = [jnp.exp2(s * score_factor - new_max * score_factor) for s in scores]
            if masked:
                weights[1] = jnp.where(is_valid, weights[1], 0.0)
            correction_factor = jnp.exp2((run_max - new_max) * score_factor)
            l_sc[:, r0:r0 + chunk] = l_sc[:, r0:r0 + chunk] * correction_factor + (
                jnp.sum(weights[0], axis=0, keepdims=True) + jnp.sum(weights[1], axis=0, keepdims=True))
            m_sc[:, r0:r0 + chunk] = new_max
            c_sc[:, r0:r0 + chunk] = correction_factor
            p_sc[:, r0:r0 + chunk] = weights[0].astype(jnp.bfloat16)
            p2_sc[:, r0:r0 + chunk] = weights[1].astype(jnp.bfloat16)
        acc_sc[...] = acc_sc[...] * c_sc[...] + (
            lax.dot_general(kv_ref[kb, 1], p_sc[...], (((0,), (0,)), ((), ())), preferred_element_type=jnp.float32)
            + lax.dot_general(kv_ref[kb + 1, 1], p2_sc[...], (((0,), (0,)), ((), ())), preferred_element_type=jnp.float32))

    def pair_body(i, carry):
        run_pair(2 * i)
        return carry
    lax.fori_loop(0, position // 2, pair_body, 0)

    @pl.when(lax.rem(position, 2) == 1)
    def _odd():
        run_pair(position - 1, masked=True)

    @pl.when(lax.rem(position, 2) == 0)
    def _even():
        run_block(position, True)

    for h in range(rows // tok):
        columns = slice(h * tok, (h + 1) * tok)
        o_ref[:, h * width:(h + 1) * width] = (acc_sc[:, columns] / l_sc[:, columns]).T.astype(o_ref.dtype)


def causal_attention(position, queries, gathered_kv, chunk=256):
    blocks, _, tok_rows, width = gathered_kv.shape
    heads = queries.shape[1] // width
    rows = heads * tok_rows
    queries_t = queries.reshape(tok_rows, heads, width).transpose(2, 1, 0).reshape(width, rows)
    kernel = functools.partial(attend_kernel, tok=tok_rows, width=width, chunk=chunk)
    return pl.pallas_call(
        kernel,
        in_specs=[pl.BlockSpec(memory_space=pltpu.SMEM)] + [pl.BlockSpec(memory_space=pltpu.VMEM)] * 2,
        out_specs=pl.BlockSpec(memory_space=pltpu.VMEM),
        out_shape=jax.ShapeDtypeStruct(queries.shape, queries.dtype),
        scratch_shapes=[
            pltpu.VMEM((tok_rows, rows), jnp.bfloat16),
            pltpu.VMEM((tok_rows, rows), jnp.bfloat16),
            pltpu.VMEM((1, rows), jnp.float32),
            pltpu.VMEM((1, rows), jnp.float32),
            pltpu.VMEM((1, rows), jnp.float32),
            pltpu.VMEM((width, rows), jnp.float32),
        ],
    )(position.reshape(1), queries_t, gathered_kv)


def shifted(block, axis, distance):
    devices = range(lax.axis_size(axis))
    route = [(i - distance, i) for i in devices if i - distance in devices]
    return lax.ppermute(block, axis, route)


def summed_over(part, axis):
    count = lax.axis_size(axis)
    total = part
    distance = 1
    while distance < count:
        route = [(i, i ^ distance) for i in range(count)]
        total = total + lax.ppermute(total, axis, route)
        distance *= 2
    return total


def packed(state, log_span):
    heads = log_span.shape[-1]
    lanes = state.shape[-1]
    rows = state.astype(jnp.bfloat16).reshape(state.shape[0], -1, lanes)
    high = lax.reduce_precision(log_span, exponent_bits=8, mantissa_bits=7)
    rest = log_span - high
    middle = lax.reduce_precision(rest, exponent_bits=8, mantissa_bits=7)
    low = rest - middle
    parts = jnp.stack((high, middle, low), axis=1).astype(jnp.bfloat16)
    tail = jnp.pad(parts, ((0, 0), (0, 16 - parts.shape[1]), (0, lanes - heads)))
    return jnp.concatenate((rows, tail), axis=1)


def unpacked(block, state_shape):
    heads = state_shape[1]
    body_rows = block.shape[1] - 16
    state = block[:, :body_rows].reshape(state_shape).astype(jnp.float32)
    parts = block[:, body_rows:body_rows + 3, :heads].astype(jnp.float32)
    return state, (parts[:, 0] + parts[:, 1]) + parts[:, 2]


def carried_scan(local_state, block_log_decay, axis, count):
    sent = packed(local_state, block_log_decay)
    one_back_state, one_back_decay = unpacked(shifted(sent, axis, 1), local_state.shape)
    two_back_state, two_back_decay = unpacked(shifted(sent, axis, 2), local_state.shape)
    state = jnp.exp(one_back_decay)[..., None, None] * two_back_state + one_back_state
    log_span = one_back_decay + two_back_decay
    distance = 2
    while distance < count:
        earlier_state, earlier_span = unpacked(
            shifted(packed(state, log_span), axis, distance), local_state.shape
        )
        state = jnp.exp(log_span)[..., None, None] * earlier_state + state
        log_span = log_span + earlier_span
        distance *= 2
    return state


def chip_carried_scan(local_state, block_log_decay):
    core = lax.axis_index("core")
    swap = [(0, 1), (1, 0)]
    sent = packed(local_state, block_log_decay)
    own_state, own_decay = unpacked(sent, local_state.shape)
    mate_state, mate_decay = unpacked(lax.ppermute(sent, "core", swap), local_state.shape)
    first_state = jnp.where(core == 0, own_state, mate_state)
    first_decay = jnp.where(core == 0, own_decay, mate_decay)
    second_state = jnp.where(core == 0, mate_state, own_state)
    second_decay = jnp.where(core == 0, mate_decay, own_decay)
    chip_state = jnp.exp(second_decay)[..., None, None] * first_state + second_state
    chip_decay = first_decay + second_decay
    half = local_state.shape[1] // 2
    chip_prefix = carried_scan(
        lax.dynamic_slice_in_dim(chip_state, core * half, half, axis=1),
        lax.dynamic_slice_in_dim(chip_decay, core * half, half, axis=1),
        "chip",
        lax.axis_size("chip"),
    )
    other_prefix = lax.ppermute(chip_prefix.astype(jnp.bfloat16), "core", swap).astype(jnp.float32)
    prefix = jnp.where(
        core == 0,
        jnp.concatenate((chip_prefix, other_prefix), axis=1),
        jnp.concatenate((other_prefix, chip_prefix), axis=1),
    )
    return jnp.where(
        core == 0, prefix, jnp.exp(first_decay)[..., None, None] * prefix + first_state
    )


def local(
    queries,
    key_rows,
    value_head_rows,
    ssm_input,
    gate_input,
    b_matrix,
    c_matrix,
    step_size,
    log_decay,
    skip_gain,
    norm_gain,
):
    tok_rows = queries.shape[0]
    position = lax.axis_index(CTX)

    gathered_kv = lax.all_gather(jnp.stack((key_rows, value_head_rows)), CTX)

    heads_local = step_size.shape[0]
    groups_local = b_matrix.shape[1] // N
    heads_group = heads_local // groups_local
    mixer_in = ssm_input.reshape(tok_rows, groups_local, heads_group, P_SIZE)
    in_maps = b_matrix.reshape(tok_rows, groups_local, N)
    out_maps = c_matrix.reshape(tok_rows, groups_local, N)
    steps_here = step_size.reshape(groups_local, heads_group, tok_rows)
    cumul = jnp.cumsum(log_decay.reshape(groups_local, heads_group, tok_rows), axis=-1)
    causal = jnp.tril(jnp.ones((tok_rows, tok_rows), dtype=bool))
    gram = jnp.einsum("tgn,sgn->gts", out_maps, in_maps, preferred_element_type=jnp.float32)
    spread = jnp.where(causal, cumul[..., :, None] - cumul[..., None, :], 0.0)
    mixing = jnp.where(
        causal, gram[:, None] * jnp.exp(spread) * steps_here[..., None, :], 0.0
    ).astype(jnp.bfloat16)
    inner = jnp.einsum("ghts,sghp->tghp", mixing, mixer_in, preferred_element_type=jnp.float32)
    weight_end = jnp.exp(cumul[..., -1:] - cumul) * steps_here
    weighted = (mixer_in * weight_end.transpose(2, 0, 1)[..., None]).astype(jnp.bfloat16)
    local_state = jnp.einsum(
        "sghp,sgn->ghpn", weighted, in_maps, preferred_element_type=jnp.float32
    )
    block_log_decay = cumul[..., -1]

    incoming = chip_carried_scan(local_state, block_log_decay)

    attention_out = causal_attention(position, queries, gathered_kv)

    carried_out = jnp.einsum(
        "ghpn,tgn->tghp", incoming, out_maps.astype(jnp.float32), precision=lax.Precision.HIGHEST
    )
    carried_out = carried_out * jnp.exp(cumul).transpose(2, 0, 1)[..., None]
    direct = skip_gain.reshape(groups_local, heads_group)[None, :, :, None] * mixer_in.astype(
        jnp.float32
    )
    outputs = (inner + carried_out + direct).reshape(tok_rows, -1)
    gated = outputs * jax.nn.silu(gate_input.astype(jnp.float32))
    square_total = summed_over(jnp.sum(gated * gated, axis=-1), "tp")
    scaling = lax.rsqrt(square_total / (STATE_HEADS * P_SIZE) + 1e-05)
    mixer_out = (gated * scaling[:, None] * norm_gain.astype(jnp.float32)).astype(jnp.bfloat16)
    return (attention_out, mixer_out)


def solution(mesh):
    placed = (
        P("ctx", "tp"),
        P("ctx", "tp"),
        P("ctx", "tp"),
        P("ctx", "tp"),
        P("ctx", "tp"),
        P("ctx", "tp"),
        P("ctx", "tp"),
        P("tp", "ctx"),
        P("tp", "ctx"),
        P("tp"),
        P("tp"),
    )
    fine_mesh = jax.sharding.Mesh(
        mesh.devices.reshape(mesh.shape["ctx"] // 2, 2, mesh.shape["tp"]), CTX + ("tp",)
    )
    placed = tuple(P(*[CTX if axis == "ctx" else axis for axis in spec]) for spec in placed)
    return jax.shard_map(
        local,
        mesh=fine_mesh,
        in_specs=placed,
        out_specs=(P(CTX, "tp"), P(CTX, "tp")),
        check_vma=False,
    )
```

```python
import functools

import jax
import jax.numpy as jnp
from jax import lax
from jax.experimental import pallas as pl
from jax.experimental.pallas import tpu as pltpu
from jax.sharding import PartitionSpec as P

HEAD_WIDTH = 128
STATE_HEADS = 128
P_SIZE = 64
N = 128


causal_score = -1e30
CTX = ("chip", "core")


def attend_kernel(pos_ref, qt_ref, kv_ref, o_ref, p_sc, m_sc, l_sc, c_sc, acc_sc, *, tok, width, chunk):
    position = pos_ref[0]
    score_factor = width ** (-0.5) * 1.4426950408889634
    rows = qt_ref.shape[1]
    block_rows = kv_ref.shape[2]
    m_sc[...] = jnp.full(m_sc.shape, causal_score, jnp.float32)
    l_sc[...] = jnp.zeros(l_sc.shape, jnp.float32)
    acc_sc[...] = jnp.zeros(acc_sc.shape, jnp.float32)

    def run_block(kb, masked):
        key_portion = kv_ref[kb, 0]
        for c in range(rows // chunk):
            r0 = c * chunk
            score_t = jnp.dot(key_portion, qt_ref[:, r0:r0 + chunk],
                              preferred_element_type=jnp.float32)
            if masked:
                key_idx = lax.broadcasted_iota(jnp.int32, (block_rows, chunk), 0)
                query_idx = (r0 % tok) + lax.broadcasted_iota(jnp.int32, (block_rows, chunk), 1)
                is_valid = key_idx <= query_idx
                score_t = jnp.where(is_valid, score_t, causal_score)
            run_max = m_sc[:, r0:r0 + chunk]
            new_max = jnp.maximum(run_max, jnp.max(score_t, axis=0, keepdims=True))
            weights = jnp.exp2(score_t * score_factor - new_max * score_factor)
            if masked:
                weights = jnp.where(is_valid, weights, 0.0)
            correction_factor = jnp.exp2((run_max - new_max) * score_factor)
            l_sc[:, r0:r0 + chunk] = l_sc[:, r0:r0 + chunk] * correction_factor + jnp.sum(weights, axis=0, keepdims=True)
            m_sc[:, r0:r0 + chunk] = new_max
            c_sc[:, r0:r0 + chunk] = correction_factor
            p_sc[:block_rows, r0:r0 + chunk] = weights.astype(jnp.bfloat16)
        acc_sc[...] = acc_sc[...] * c_sc[...] + lax.dot_general(kv_ref[kb, 1], p_sc[:block_rows], (((0,), (0,)), ((), ())), preferred_element_type=jnp.float32)

    def run_pair(kb):
        keys = (kv_ref[kb, 0], kv_ref[kb + 1, 0])
        for c in range(rows // chunk):
            r0 = c * chunk
            scores = [jnp.dot(k, qt_ref[:, r0:r0 + chunk], preferred_element_type=jnp.float32) for k in keys]
            run_max = m_sc[:, r0:r0 + chunk]
            block_max = jnp.maximum(jnp.max(scores[0], axis=0, keepdims=True), jnp.max(scores[1], axis=0, keepdims=True))
            new_max = jnp.maximum(run_max, block_max)
            weights = [jnp.exp2(s * score_factor - new_max * score_factor) for s in scores]
            correction_factor = jnp.exp2((run_max - new_max) * score_factor)
            l_sc[:, r0:r0 + chunk] = l_sc[:, r0:r0 + chunk] * correction_factor + (
                jnp.sum(weights[0], axis=0, keepdims=True) + jnp.sum(weights[1], axis=0, keepdims=True))
            m_sc[:, r0:r0 + chunk] = new_max
            c_sc[:, r0:r0 + chunk] = correction_factor
            p_sc[:block_rows, r0:r0 + chunk] = weights[0].astype(jnp.bfloat16)
            p_sc[block_rows:, r0:r0 + chunk] = weights[1].astype(jnp.bfloat16)
        pair_values = kv_ref[pl.ds(kb, 2), 1].reshape(2 * block_rows, width)
        acc_sc[...] = acc_sc[...] * c_sc[...] + lax.dot_general(
            pair_values, p_sc[...], (((0,), (0,)), ((), ())), preferred_element_type=jnp.float32)

    def pair_body(i, carry):
        run_pair(2 * i)
        return carry
    lax.fori_loop(0, position // 2, pair_body, 0)

    @pl.when(lax.rem(position, 2) == 1)
    def _odd():
        run_block(position - 1, False)

    run_block(position, True)
    for h in range(rows // tok):
        columns = slice(h * tok, (h + 1) * tok)
        o_ref[:, h * width:(h + 1) * width] = (acc_sc[:, columns] / l_sc[:, columns]).T.astype(o_ref.dtype)


def causal_attention(position, queries, gathered_kv, chunk=256):
    blocks, _, tok_rows, width = gathered_kv.shape
    heads = queries.shape[1] // width
    rows = heads * tok_rows
    queries_t = queries.reshape(tok_rows, heads, width).transpose(2, 1, 0).reshape(width, rows)
    kernel = functools.partial(attend_kernel, tok=tok_rows, width=width, chunk=chunk)
    return pl.pallas_call(
        kernel,
        in_specs=[pl.BlockSpec(memory_space=pltpu.SMEM)] + [pl.BlockSpec(memory_space=pltpu.VMEM)] * 2,
        out_specs=pl.BlockSpec(memory_space=pltpu.VMEM),
        out_shape=jax.ShapeDtypeStruct(queries.shape, queries.dtype),
        scratch_shapes=[
            pltpu.VMEM((2 * tok_rows, rows), jnp.bfloat16),
            pltpu.VMEM((1, rows), jnp.float32),
            pltpu.VMEM((1, rows), jnp.float32),
            pltpu.VMEM((1, rows), jnp.float32),
            pltpu.VMEM((width, rows), jnp.float32),
        ],
    )(position.reshape(1), queries_t, gathered_kv)


def shifted(block, axis, distance):
    devices = range(lax.axis_size(axis))
    route = [(i - distance, i) for i in devices if i - distance in devices]
    return lax.ppermute(block, axis, route)


def summed_over(part, axis):
    count = lax.axis_size(axis)
    total = part
    distance = 1
    while distance < count:
        route = [(i, i ^ distance) for i in range(count)]
        total = total + lax.ppermute(total, axis, route)
        distance *= 2
    return total


def packed(state, log_span):
    heads = log_span.shape[-1]
    lanes = state.shape[-1]
    rows = state.astype(jnp.bfloat16).reshape(state.shape[0], -1, lanes)
    high = lax.reduce_precision(log_span, exponent_bits=8, mantissa_bits=7)
    rest = log_span - high
    middle = lax.reduce_precision(rest, exponent_bits=8, mantissa_bits=7)
    low = rest - middle
    parts = jnp.stack((high, middle, low), axis=1).astype(jnp.bfloat16)
    tail = jnp.pad(parts, ((0, 0), (0, 16 - parts.shape[1]), (0, lanes - heads)))
    return jnp.concatenate((rows, tail), axis=1)


def unpacked(block, state_shape):
    heads = state_shape[1]
    body_rows = block.shape[1] - 16
    state = block[:, :body_rows].reshape(state_shape).astype(jnp.float32)
    parts = block[:, body_rows:body_rows + 3, :heads].astype(jnp.float32)
    return state, (parts[:, 0] + parts[:, 1]) + parts[:, 2]


def carried_scan(local_state, block_log_decay, axis, count):
    sent = packed(local_state, block_log_decay)
    one_back_state, one_back_decay = unpacked(shifted(sent, axis, 1), local_state.shape)
    two_back_state, two_back_decay = unpacked(shifted(sent, axis, 2), local_state.shape)
    state = jnp.exp(one_back_decay)[..., None, None] * two_back_state + one_back_state
    log_span = one_back_decay + two_back_decay
    distance = 2
    while distance < count:
        earlier_state, earlier_span = unpacked(
            shifted(packed(state, log_span), axis, distance), local_state.shape
        )
        state = jnp.exp(log_span)[..., None, None] * earlier_state + state
        log_span = log_span + earlier_span
        distance *= 2
    return state


def chip_carried_scan(local_state, block_log_decay):
    core = lax.axis_index("core")
    swap = [(0, 1), (1, 0)]
    sent = packed(local_state, block_log_decay)
    own_state, own_decay = unpacked(sent, local_state.shape)
    mate_state, mate_decay = unpacked(lax.ppermute(sent, "core", swap), local_state.shape)
    first_state = jnp.where(core == 0, own_state, mate_state)
    first_decay = jnp.where(core == 0, own_decay, mate_decay)
    second_state = jnp.where(core == 0, mate_state, own_state)
    second_decay = jnp.where(core == 0, mate_decay, own_decay)
    chip_state = jnp.exp(second_decay)[..., None, None] * first_state + second_state
    chip_decay = first_decay + second_decay
    half = local_state.shape[1] // 2
    chip_prefix = carried_scan(
        lax.dynamic_slice_in_dim(chip_state, core * half, half, axis=1),
        lax.dynamic_slice_in_dim(chip_decay, core * half, half, axis=1),
        "chip",
        lax.axis_size("chip"),
    )
    other_prefix = lax.ppermute(chip_prefix.astype(jnp.bfloat16), "core", swap).astype(jnp.float32)
    prefix = jnp.where(
        core == 0,
        jnp.concatenate((chip_prefix, other_prefix), axis=1),
        jnp.concatenate((other_prefix, chip_prefix), axis=1),
    )
    return jnp.where(
        core == 0, prefix, jnp.exp(first_decay)[..., None, None] * prefix + first_state
    )


def local(
    queries,
    key_rows,
    value_head_rows,
    ssm_input,
    gate_input,
    b_matrix,
    c_matrix,
    step_size,
    log_decay,
    skip_gain,
    norm_gain,
):
    tok_rows = queries.shape[0]
    position = lax.axis_index(CTX)

    gathered_kv = lax.all_gather(jnp.stack((key_rows, value_head_rows)), CTX)

    heads_local = step_size.shape[0]
    groups_local = b_matrix.shape[1] // N
    heads_group = heads_local // groups_local
    mixer_in = ssm_input.reshape(tok_rows, groups_local, heads_group, P_SIZE)
    in_maps = b_matrix.reshape(tok_rows, groups_local, N)
    out_maps = c_matrix.reshape(tok_rows, groups_local, N)
    steps_here = step_size.reshape(groups_local, heads_group, tok_rows)
    cumul = jnp.cumsum(log_decay.reshape(groups_local, heads_group, tok_rows), axis=-1)
    causal = jnp.tril(jnp.ones((tok_rows, tok_rows), dtype=bool))
    gram = jnp.einsum("tgn,sgn->gts", out_maps, in_maps, preferred_element_type=jnp.float32)
    spread = jnp.where(causal, cumul[..., :, None] - cumul[..., None, :], 0.0)
    mixing = jnp.where(
        causal, gram[:, None] * jnp.exp(spread) * steps_here[..., None, :], 0.0
    ).astype(jnp.bfloat16)
    inner = jnp.einsum("ghts,sghp->tghp", mixing, mixer_in, preferred_element_type=jnp.float32)
    weight_end = jnp.exp(cumul[..., -1:] - cumul) * steps_here
    weighted = (mixer_in * weight_end.transpose(2, 0, 1)[..., None]).astype(jnp.bfloat16)
    local_state = jnp.einsum(
        "sghp,sgn->ghpn", weighted, in_maps, preferred_element_type=jnp.float32
    )
    block_log_decay = cumul[..., -1]

    incoming = chip_carried_scan(local_state, block_log_decay)

    attention_out = causal_attention(position, queries, gathered_kv)

    carried_out = jnp.einsum(
        "ghpn,tgn->tghp", incoming, out_maps.astype(jnp.float32), precision=lax.Precision.HIGHEST
    )
    carried_out = carried_out * jnp.exp(cumul).transpose(2, 0, 1)[..., None]
    direct = skip_gain.reshape(groups_local, heads_group)[None, :, :, None] * mixer_in.astype(
        jnp.float32
    )
    outputs = (inner + carried_out + direct).reshape(tok_rows, -1)
    gated = outputs * jax.nn.silu(gate_input.astype(jnp.float32))
    square_total = summed_over(jnp.sum(gated * gated, axis=-1), "tp")
    scaling = lax.rsqrt(square_total / (STATE_HEADS * P_SIZE) + 1e-05)
    mixer_out = (gated * scaling[:, None] * norm_gain.astype(jnp.float32)).astype(jnp.bfloat16)
    return (attention_out, mixer_out)


def solution(mesh):
    placed = (
        P("ctx", "tp"),
        P("ctx", "tp"),
        P("ctx", "tp"),
        P("ctx", "tp"),
        P("ctx", "tp"),
        P("ctx", "tp"),
        P("ctx", "tp"),
        P("tp", "ctx"),
        P("tp", "ctx"),
        P("tp"),
        P("tp"),
    )
    fine_mesh = jax.sharding.Mesh(
        mesh.devices.reshape(mesh.shape["ctx"] // 2, 2, mesh.shape["tp"]), CTX + ("tp",)
    )
    placed = tuple(P(*[CTX if axis == "ctx" else axis for axis in spec]) for spec in placed)
    return jax.shard_map(
        local,
        mesh=fine_mesh,
        in_specs=placed,
        out_specs=(P(CTX, "tp"), P(CTX, "tp")),
        check_vma=False,
    )
```
